512 devices in a mesh: req: 64 (over x, y, core), tp: 8 (over z).
Axes of the slice: x: 4, y: 8, z: 8, core: 2. Of those that a mesh axis runs over, the one named last changes fastest.
Arguments:
- vit_context: bfloat16 [32768, 4096], P('req', 'tp'), may hold values from -6 to 6
- vision_residual: bfloat16 [32768, 4096], P('req', 'tp'), may hold values from -75 to 75
- out_weight: bfloat16 [4096, 4096], P('tp', 'req'), may hold values from -0.09375 to 0.09375
- layer_scale: float32 [4096], P('tp'), may hold values from 0.2 to 2
- prompt: bfloat16 [64, 256, 4096], P('req', None, 'tp'), may hold values from -75 to 75
- prompt_len: int32 [64], P('req'), may hold values from 128 to 256
- image_at: int32 [64], P('req'), may hold values from 0 to 128
- grid_sizes: int32 [128, 2], replicated, may hold values from 7 to 8, as said below
- image_owner: int32 [128], replicated, may hold values from 0 to 63, as said below
- norm_gain: float32 [4096], replicated, may hold values from 0.5 to 1.5
- qkv_weight: bfloat16 [4096, 6144], P('req', 'tp'), may hold values from -0.09375 to 0.09375
Outputs:
- qkv: bfloat16 [24576, 6144], P('req', 'tp')
The draws below stay inside these ranges and needn't reach their ends.
Inputs may be any that keep to these rules, and one draw needn't show every extreme that they name: `image_owner`: each request owns exactly 2 images. `grid_sizes`: each side is 7 or 8; in every draw the images of some request are all 8 by 8, so that request has exactly 128 merged rows.
All inputs are finite; a program needn't handle non-finite values.
Results may differ from the reference program's by a relative error of at most 0.008.
Values may be sent and summed in bfloat16 or wider, within the bound.
No kernel may reach another device: no remote copies, remote signals or barrier semaphores. Data moves between devices by JAX's collectives and lax.ppermute only.
A program may use at most 64 MiB of HBM per device.

```python
import math
import jax
import jax.numpy as jnp
from jax import lax

D = 4096
HEAD = 128
GRID_MAX = 8
IMG_REQ = 2
PROMPT_MAX = 256
GROUP = 4
QKV = 6144
IMG_MAX = 128
MRG_DEV = 128
P_DEV = 512
SEQ = 384
REQS = 64
IMAGES = 128
PATCHES = 32768
N_TP = 8


def image_plan(key):
    order = jax.random.permutation(jax.random.fold_in(key, 11), IMAGES)
    image_owner = (order // IMG_REQ).astype(jnp.int32)
    chosen = jax.random.randint(jax.random.fold_in(key, 12), (), 0, REQS)
    sides = jax.random.randint(jax.random.fold_in(key, 13), (IMAGES, 2), GRID_MAX - 1, GRID_MAX + 1)
    sides = jnp.where((image_owner == chosen)[:, None], GRID_MAX, sides)
    return (image_owner, sides.astype(jnp.int32))


def draw_image_owner(key, part):
    return image_plan(key)[0]


def draw_grid_sizes(key, part):
    return image_plan(key)[1]


def scaled_rows(key, array_shape):
    key_list = jax.random.split(key, 3)
    raw_values = jax.random.normal(key_list[0], array_shape, jnp.float32)
    raw_values = jnp.clip(raw_values, -5.0, 5.0)
    row_draw = jax.random.uniform(key_list[1], array_shape[:-1] + (1,), jnp.float32)
    row_scale = jnp.exp(math.log(10.0) * (row_draw - 0.5))
    column_draw = jax.random.uniform(key_list[2], (array_shape[-1],), jnp.float32)
    column_scale = jnp.exp(math.log(10.0) * (column_draw - 0.5))
    return raw_values * row_scale * column_scale


def draw_prompt(key, part):
    return scaled_rows(key, (REQS, PROMPT_MAX, D)).astype(jnp.bfloat16)


def draw_vision_residual(key, part):
    return scaled_rows(key, (PATCHES, D)).astype(jnp.bfloat16)


def set_ends(array, rng, smallest, largest):
    shape = array.shape
    index_at = [jax.random.randint(jax.random.fold_in(rng, axis), (), 0, shape[axis]) for axis in range(len(shape))]
    array = array.at[tuple(index_at)].set(smallest)
    longest = shape.index(max(shape))
    index_at[longest] = (index_at[longest] + 1) % shape[longest]
    return array.at[tuple(index_at)].set(largest)


def block_levels(rng, shape, cuts, least, largest):
    def one(position, blocks):
        heights = jax.random.uniform(jax.random.fold_in(jax.random.fold_in(rng, 6), position), (blocks,), jnp.float32, least / len(cuts), largest / len(cuts))
        return jnp.repeat(jnp.exp(heights), shape[position] // blocks).reshape((-1,) + (1,) * (len(shape) - position - 1))

    factor_of = one(*cuts[0])
    for cut in cuts[1:]:
        factor_of = factor_of * one(*cut)
    return factor_of


def noise(rng, dims, width, bound, cuts=(), kind=jnp.bfloat16):
    drawn = width * jax.random.normal(rng, dims, jnp.float32)
    if cuts:
        drawn = drawn * block_levels(rng, dims, cuts, -0.22, 0.18)
    return jnp.clip(drawn, -bound, bound).astype(kind)


def setup_inputs(seed: int = 0) -> dict:
    seeds = jax.random.split(jax.random.key(seed), 12)
    return {
        "vit_context": noise(seeds[0], (PATCHES, D), 1.0, 6.0, ((0, 64), (1, 8))),
        "vision_residual": draw_vision_residual(jax.random.fold_in(seeds[11], 71), 0),
        "out_weight": noise(seeds[2], (D, D), D ** -0.5, 0.09375, ((0, 8), (1, 64))),
        "layer_scale": jnp.clip(jnp.exp(math.log(2.0) - 2.3025851 * jax.random.uniform(seeds[3], (D,), jnp.float32) ** block_levels(seeds[3], (D,), ((0, 8),), -0.2, 0.2)), 0.2, 2.0),
        "prompt": draw_prompt(jax.random.fold_in(seeds[11], 71), 0),
        "prompt_len": set_ends(jax.random.randint(seeds[5], (REQS,), PROMPT_MAX // 2, PROMPT_MAX + 1), jax.random.fold_in(seeds[5], 1), PROMPT_MAX // 2, PROMPT_MAX).astype(jnp.int32),
        "image_at": set_ends(jax.random.randint(seeds[6], (REQS,), 0, PROMPT_MAX // 2 + 1), jax.random.fold_in(seeds[6], 1), 0, (PROMPT_MAX // 2 + 1) - 1).astype(jnp.int32),
        "grid_sizes": draw_grid_sizes(jax.random.fold_in(seeds[11], 71), 0),
        "image_owner": draw_image_owner(jax.random.fold_in(seeds[11], 71), 0),
        "norm_gain": jnp.clip(1.0 + 0.1 * jax.random.normal(seeds[9], (D,), jnp.float32), 0.5, 1.5),
        "qkv_weight": noise(seeds[10], (D, QKV), D ** -0.5, 0.09375, ((0, 64), (1, 8))),
    }


def request_plan(grid_sizes, image_owner, requests):
    image_rows = grid_sizes[:, 0] * grid_sizes[:, 1]
    member = (image_owner[:, None] == jnp.arange(requests, dtype=jnp.int32)[None, :]).astype(jnp.int32)
    counts = lax.optimization_barrier(jnp.sum(image_rows[:, None] * member, axis=0)).astype(jnp.int32)
    starts = (jnp.cumsum(counts) - counts).astype(jnp.int32)
    return (counts, starts)

def rope_tables(count):
    half_size = HEAD // 2
    exponent = jnp.arange(half_size, dtype=jnp.float32) * (2.0 / HEAD)
    frequency = jnp.exp(-exponent * jnp.log(jnp.float32(500000.0)))
    angles = jnp.arange(count, dtype=jnp.float32)[:, None] * frequency[None, :]
    return (jnp.cos(angles), jnp.sin(angles))

def apply_rope(projected, cosine_table, sine_table):
    seq_rows = projected.shape[0]
    head_blocks = projected.reshape(seq_rows, -1, GROUP + 2, HEAD)
    turning = head_blocks[:, :, :GROUP + 1, :]
    first_half = turning[..., :HEAD // 2]
    second_half = turning[..., HEAD // 2:]
    cosine_wide = cosine_table[:, None, None, :]
    sine_wide = sine_table[:, None, None, :]
    turned = jnp.concatenate([first_half * cosine_wide - second_half * sine_wide, second_half * cosine_wide + first_half * sine_wide], axis=-1)
    head_blocks = jnp.concatenate([turned, head_blocks[:, :, GROUP + 1:, :]], axis=2)
    return head_blocks.reshape(seq_rows, -1)

def normalize(embedded, norm_gain):
    values = embedded.astype(jnp.float32)
    mean_square = lax.optimization_barrier(jnp.mean(values * values, axis=-1, keepdims=True))
    return (values * lax.rsqrt(mean_square + 1e-05) * norm_gain[None, :]).astype(jnp.bfloat16)

def reference(vit_context, vision_residual, out_weight, layer_scale, prompt, prompt_len, image_at, grid_sizes, image_owner, norm_gain, qkv_weight):
    block_width = D // N_TP

    def vision_block(block_item):
        context_rows, residual_rows = block_item
        merged_context = lax.optimization_barrier(jnp.mean(context_rows.astype(jnp.float32).reshape(MRG_DEV, 4, D), axis=1)).astype(jnp.bfloat16)
        merged_residual = lax.optimization_barrier(jnp.mean(residual_rows.astype(jnp.float32).reshape(MRG_DEV, 4, D), axis=1))
        running = jnp.zeros((MRG_DEV, D), jnp.float32)
        for part_index in range(N_TP):
            column_start = part_index * block_width
            block_term = jnp.dot(merged_context[:, column_start:column_start + block_width], out_weight[column_start:column_start + block_width, :], preferred_element_type=jnp.float32)
            rounded = lax.optimization_barrier(block_term.astype(jnp.bfloat16))
            running = running + rounded.astype(jnp.float32)
        return (merged_residual + layer_scale[None, :] * running).astype(jnp.bfloat16)
    merged_blocks = lax.map(vision_block, (vit_context.reshape(REQS, P_DEV, D), vision_residual.reshape(REQS, P_DEV, D)))
    merged = jnp.transpose(merged_blocks, (1, 0, 2)).reshape(MRG_DEV * REQS, D)
    padded = jnp.concatenate([merged, jnp.zeros((IMG_MAX, D), merged.dtype)], axis=0)
    counts, starts = request_plan(grid_sizes, image_owner, REQS)
    cosine_table, sine_table = rope_tables(SEQ)

    def one_request(request_item):
        prompt_rows, own_count, own_start, prompt_count, image_from = request_item
        image_rows = lax.dynamic_slice_in_dim(padded, own_start.astype(jnp.int32), IMG_MAX, 0)
        slot_index = jnp.arange(SEQ, dtype=jnp.int32)
        image_row = slot_index - image_from
        in_image = (image_row >= 0) & (image_row < own_count)
        is_live = slot_index < prompt_count + own_count
        from_prompt = is_live & jnp.logical_not(in_image)
        prompt_row = jnp.where(slot_index < image_from, slot_index, slot_index - own_count)
        image_choice = jnp.take(image_rows, jnp.clip(image_row, 0, IMG_MAX - 1).astype(jnp.int32), axis=0)
        prompt_choice = jnp.take(prompt_rows, jnp.clip(prompt_row, 0, PROMPT_MAX - 1).astype(jnp.int32), axis=0)
        embedded = jnp.where(in_image[:, None], image_choice, jnp.where(from_prompt[:, None], prompt_choice, jnp.zeros_like(prompt_choice)))
        normed = normalize(embedded, norm_gain)
        projected = jnp.dot(normed, qkv_weight, preferred_element_type=jnp.float32)
        return apply_rope(projected, cosine_table, sine_table).astype(jnp.bfloat16)
    outputs = lax.map(one_request, (prompt, counts, starts, prompt_len, image_at))
    return outputs.reshape(REQS * SEQ, QKV)
```

```python
import jax
import jax.numpy as jnp
from jax import lax
from jax.sharding import PartitionSpec as P

HEAD = 128
GROUP = 4
IMG_MAX = 128


def request_plan(grid_sizes, image_owner, requests):
    image_rows = grid_sizes[:, 0] * grid_sizes[:, 1]
    member = (image_owner[:, None] == jnp.arange(requests, dtype=jnp.int32)[None, :]).astype(
        jnp.int32
    )
    counts = jnp.sum(image_rows[:, None] * member, axis=0)
    starts = jnp.cumsum(counts) - counts
    return (counts, starts)


def rope_tables(count):
    half_size = HEAD // 2
    exponent = jnp.arange(half_size, dtype=jnp.float32) * (2.0 / HEAD)
    frequency = jnp.exp(-exponent * jnp.log(jnp.float32(500000.0)))
    angles = jnp.arange(count, dtype=jnp.float32)[:, None] * frequency[None, :]
    return (jnp.cos(angles), jnp.sin(angles))


def apply_rope(projected, cosine_table, sine_table):
    seq_rows = projected.shape[0]
    head_blocks = projected.reshape(seq_rows, -1, GROUP + 2, HEAD)
    turning = head_blocks[:, :, : GROUP + 1, :]
    first_half = turning[..., : HEAD // 2]
    second_half = turning[..., HEAD // 2 :]
    cosine_wide = cosine_table[:, None, None, :]
    sine_wide = sine_table[:, None, None, :]
    turned = jnp.concatenate(
        [
            first_half * cosine_wide - second_half * sine_wide,
            second_half * cosine_wide + first_half * sine_wide,
        ],
        axis=-1,
    )
    head_blocks = jnp.concatenate([turned, head_blocks[:, :, GROUP + 1 :, :]], axis=2)
    return head_blocks.reshape(seq_rows, -1)


def normalize(embedded, norm_gain):
    values = embedded.astype(jnp.float32)
    mean_square = jnp.mean(values * values, axis=-1, keepdims=True)
    return (values * lax.rsqrt(mean_square + 1e-05) * norm_gain[None, :]).astype(jnp.bfloat16)


def shards(
    vit_context,
    vision_residual,
    out_weight,
    layer_scale,
    prompt,
    prompt_len,
    image_at,
    grid_sizes,
    image_owner,
    norm_gain,
    qkv_weight,
):
    requests = lax.axis_size("req")
    device_index = lax.axis_index("req")
    feature_width = vit_context.shape[1]
    merged_context = jnp.mean(
        vit_context.astype(jnp.float32).reshape(-1, 4, feature_width), axis=1
    ).astype(jnp.bfloat16)
    merged_residual = jnp.mean(
        vision_residual.astype(jnp.float32).reshape(-1, 4, feature_width), axis=1
    )
    partial_value = jnp.dot(
        merged_context,
        lax.all_gather(out_weight, "req", axis=1, tiled=True),
        preferred_element_type=jnp.float32,
    )
    tp_count = lax.axis_size("tp")
    block_terms = partial_value.astype(jnp.bfloat16).reshape(
        -1, tp_count, feature_width
    ).transpose(1, 0, 2)
    own_share = jnp.sum(
        lax.all_to_all(block_terms, "tp", 0, 0, tiled=True).astype(jnp.float32), axis=0
    )
    merged = (merged_residual + layer_scale[None, :] * own_share).astype(jnp.bfloat16)
    merged_count = merged.shape[0]
    counts, starts = request_plan(grid_sizes, image_owner, requests)
    request_ends = starts + counts
    capacity = (IMG_MAX + requests - 1) // requests
    request_ids = jnp.arange(requests, dtype=jnp.int32)
    group_index = jnp.arange(merged_count, dtype=jnp.int32) * requests + device_index
    destination = jnp.sum((request_ends[None, :] <= group_index[:, None]).astype(jnp.int32), axis=1)
    owned_start = jnp.sum(
        jnp.where(destination[:, None] == request_ids[None, :], starts[None, :], 0), axis=1
    )
    target = destination * capacity + (group_index - owned_start) // requests
    usable = destination < requests
    send_slots = jnp.arange(requests * capacity, dtype=jnp.int32)
    placing = ((send_slots[:, None] == target[None, :]) & usable[None, :]).astype(jnp.bfloat16)
    outgoing = jnp.dot(placing, merged, preferred_element_type=jnp.float32).astype(jnp.bfloat16)
    arrived = lax.all_to_all(
        outgoing.reshape(requests, capacity, feature_width),
        "req",
        split_axis=0,
        concat_axis=0,
        tiled=True,
    )
    arrived = arrived.reshape(requests * capacity, feature_width)
    own_request = request_ids == device_index
    own_count = jnp.sum(jnp.where(own_request, counts, 0))
    own_start = jnp.sum(jnp.where(own_request, starts, 0))
    image_from = image_at[0]
    prompt_count = prompt_len[0]
    seq_slots = prompt.shape[1] + IMG_MAX
    slot_index = jnp.arange(seq_slots, dtype=jnp.int32)
    image_row = slot_index - image_from
    in_image = (image_row >= 0) & (image_row < own_count)
    is_live = slot_index < prompt_count + own_count
    from_prompt = is_live & jnp.logical_not(in_image)
    flat_index = (own_start + image_row) % requests * capacity + image_row // requests
    image_pick = ((flat_index[:, None] == send_slots[None, :]) & in_image[:, None]).astype(
        jnp.bfloat16
    )
    prompt_row = jnp.where(slot_index < image_from, slot_index, slot_index - own_count)
    prompt_ids = jnp.arange(prompt.shape[1], dtype=jnp.int32)
    prompt_pick = ((prompt_row[:, None] == prompt_ids[None, :]) & from_prompt[:, None]).astype(
        jnp.bfloat16
    )
    embedded = (
        jnp.dot(image_pick, arrived, preferred_element_type=jnp.float32)
        + jnp.dot(prompt_pick, prompt[0], preferred_element_type=jnp.float32)
    ).astype(jnp.bfloat16)
    full_weight = lax.all_gather(qkv_weight, "req", axis=0, tiled=True)
    embedded, full_weight = lax.optimization_barrier((embedded, full_weight))
    gathered = lax.all_gather(embedded, "tp", axis=1, tiled=True)
    normed = normalize(gathered, norm_gain)
    projected = jnp.dot(normed, full_weight, preferred_element_type=jnp.float32)
    cosine_table, sine_table = rope_tables(seq_slots)
    return apply_rope(projected, cosine_table, sine_table).astype(jnp.bfloat16)


def solution(mesh):
    in_specs = (
        P("req", "tp"),
        P("req", "tp"),
        P("tp", "req"),
        P("tp"),
        P("req", None, "tp"),
        P("req"),
        P("req"),
        P(),
        P(),
        P(),
        P("req", "tp"),
    )
    out_specs = P("req", "tp")
    return jax.shard_map(shards, mesh=mesh, in_specs=in_specs, out_specs=out_specs, check_vma=False)
```

```python
import jax
import jax.numpy as jnp
from jax import lax
from jax.sharding import PartitionSpec as P

HEAD = 128
GROUP = 4
IMG_MAX = 128


def request_plan(grid_sizes, image_owner, requests):
    image_rows = grid_sizes[:, 0] * grid_sizes[:, 1]
    member = (image_owner[:, None] == jnp.arange(requests, dtype=jnp.int32)[None, :]).astype(
        jnp.int32
    )
    counts = jnp.sum(image_rows[:, None] * member, axis=0)
    starts = jnp.cumsum(counts) - counts
    return (counts, starts)


def rope_tables(count):
    half_size = HEAD // 2
    exponent = jnp.arange(half_size, dtype=jnp.float32) * (2.0 / HEAD)
    frequency = jnp.exp(-exponent * jnp.log(jnp.float32(500000.0)))
    angles = jnp.arange(count, dtype=jnp.float32)[:, None] * frequency[None, :]
    return (jnp.cos(angles), jnp.sin(angles))


def apply_rope(projected, cosine_table, sine_table):
    seq_rows = projected.shape[0]
    head_blocks = projected.reshape(seq_rows, -1, GROUP + 2, HEAD)
    turning = head_blocks[:, :, : GROUP + 1, :]
    first_half = turning[..., : HEAD // 2]
    second_half = turning[..., HEAD // 2 :]
    cosine_wide = cosine_table[:, None, None, :]
    sine_wide = sine_table[:, None, None, :]
    turned = jnp.concatenate(
        [
            first_half * cosine_wide - second_half * sine_wide,
            second_half * cosine_wide + first_half * sine_wide,
        ],
        axis=-1,
    )
    head_blocks = jnp.concatenate([turned, head_blocks[:, :, GROUP + 1 :, :]], axis=2)
    return head_blocks.reshape(seq_rows, -1)


def normalize(embedded, norm_gain):
    values = embedded.astype(jnp.float32)
    mean_square = jnp.mean(values * values, axis=-1, keepdims=True)
    return (values * lax.rsqrt(mean_square + 1e-05) * norm_gain[None, :]).astype(jnp.bfloat16)


def gather_features(rows, tp_count):
    copies = jnp.broadcast_to(rows[None], (tp_count,) + rows.shape)
    blocks = lax.all_to_all(copies, "tp", 0, 0, tiled=True)
    return blocks.transpose(1, 0, 2).reshape(rows.shape[0], -1)


def shards(
    vit_context,
    vision_residual,
    out_weight,
    layer_scale,
    prompt,
    prompt_len,
    image_at,
    grid_sizes,
    image_owner,
    norm_gain,
    qkv_weight,
):
    requests = lax.axis_size("req")
    device_index = lax.axis_index("req")
    feature_width = vit_context.shape[1]
    merged_context = jnp.mean(
        vit_context.astype(jnp.float32).reshape(-1, 4, feature_width), axis=1
    ).astype(jnp.bfloat16)
    merged_residual = jnp.mean(
        vision_residual.astype(jnp.float32).reshape(-1, 4, feature_width), axis=1
    )
    full_prompt = gather_features(prompt[0], lax.axis_size("tp"))
    full_prompt, merged_context = lax.optimization_barrier((full_prompt, merged_context))
    partial_value = jnp.dot(
        merged_context,
        lax.all_gather(out_weight, "req", axis=1, tiled=True),
        preferred_element_type=jnp.float32,
    )
    tp_count = lax.axis_size("tp")
    block_terms = partial_value.astype(jnp.bfloat16).reshape(
        -1, tp_count, feature_width
    ).transpose(1, 0, 2)
    own_share = jnp.sum(
        lax.all_to_all(block_terms, "tp", 0, 0, tiled=True).astype(jnp.float32), axis=0
    )
    merged = (merged_residual + layer_scale[None, :] * own_share).astype(jnp.bfloat16)
    merged_count = merged.shape[0]
    counts, starts = request_plan(grid_sizes, image_owner, requests)
    request_ends = starts + counts
    capacity = (IMG_MAX + requests - 1) // requests
    request_ids = jnp.arange(requests, dtype=jnp.int32)
    group_index = jnp.arange(merged_count, dtype=jnp.int32) * requests + device_index
    destination = jnp.sum((request_ends[None, :] <= group_index[:, None]).astype(jnp.int32), axis=1)
    owned_start = jnp.sum(
        jnp.where(destination[:, None] == request_ids[None, :], starts[None, :], 0), axis=1
    )
    target = destination * capacity + (group_index - owned_start) // requests
    usable = destination < requests
    send_slots = jnp.arange(requests * capacity, dtype=jnp.int32)
    placing = ((send_slots[:, None] == target[None, :]) & usable[None, :]).astype(jnp.bfloat16)
    outgoing = jnp.dot(placing, merged, preferred_element_type=jnp.float32).astype(jnp.bfloat16)
    arrived = lax.all_to_all(
        outgoing.reshape(requests, capacity, feature_width),
        "req",
        split_axis=0,
        concat_axis=0,
        tiled=True,
    )
    arrived = arrived.reshape(requests * capacity, feature_width)
    own_request = request_ids == device_index
    own_count = jnp.sum(jnp.where(own_request, counts, 0))
    own_start = jnp.sum(jnp.where(own_request, starts, 0))
    image_from = image_at[0]
    prompt_count = prompt_len[0]
    seq_slots = prompt.shape[1] + IMG_MAX
    slot_index = jnp.arange(seq_slots, dtype=jnp.int32)
    image_row = slot_index - image_from
    in_image = (image_row >= 0) & (image_row < own_count)
    is_live = slot_index < prompt_count + own_count
    from_prompt = is_live & jnp.logical_not(in_image)
    flat_index = (own_start + image_row) % requests * capacity + image_row // requests
    image_pick = ((flat_index[:, None] == send_slots[None, :]) & in_image[:, None]).astype(
        jnp.bfloat16
    )
    prompt_row = jnp.where(slot_index < image_from, slot_index, slot_index - own_count)
    prompt_ids = jnp.arange(prompt.shape[1], dtype=jnp.int32)
    prompt_pick = ((prompt_row[:, None] == prompt_ids[None, :]) & from_prompt[:, None]).astype(
        jnp.bfloat16
    )
    full_image = gather_features(arrived, tp_count)
    embedded = (
        jnp.dot(image_pick, full_image, preferred_element_type=jnp.float32)
        + jnp.dot(prompt_pick, full_prompt, preferred_element_type=jnp.float32)
    ).astype(jnp.bfloat16)
    full_weight = lax.all_gather(qkv_weight, "req", axis=0, tiled=True)
    normed = normalize(embedded, norm_gain)
    projected = jnp.dot(normed, full_weight, preferred_element_type=jnp.float32)
    cosine_table, sine_table = rope_tables(seq_slots)
    return apply_rope(projected, cosine_table, sine_table).astype(jnp.bfloat16)


def solution(mesh):
    in_specs = (
        P("req", "tp"),
        P("req", "tp"),
        P("tp", "req"),
        P("tp"),
        P("req", None, "tp"),
        P("req"),
        P("req"),
        P(),
        P(),
        P(),
        P("req", "tp"),
    )
    out_specs = P("req", "tp")
    return jax.shard_map(shards, mesh=mesh, in_specs=in_specs, out_specs=out_specs, check_vma=False)
```

```python
import jax
import jax.numpy as jnp
from jax import lax
from jax.sharding import Mesh, PartitionSpec as P

HEAD = 128
GROUP = 4
IMG_MAX = 128
REQ = ("rxy", "rc")


def request_plan(grid_sizes, image_owner, requests):
    image_rows = grid_sizes[:, 0] * grid_sizes[:, 1]
    member = (image_owner[:, None] == jnp.arange(requests, dtype=jnp.int32)[None, :]).astype(
        jnp.int32
    )
    counts = jnp.sum(image_rows[:, None] * member, axis=0)
    starts = jnp.cumsum(counts) - counts
    return (counts, starts)


def rope_tables(count):
    half_size = HEAD // 2
    exponent = jnp.arange(half_size, dtype=jnp.float32) * (2.0 / HEAD)
    frequency = jnp.exp(-exponent * jnp.log(jnp.float32(500000.0)))
    angles = jnp.arange(count, dtype=jnp.float32)[:, None] * frequency[None, :]
    return (jnp.cos(angles), jnp.sin(angles))


def apply_rope(projected, cosine_table, sine_table):
    seq_rows = projected.shape[0]
    head_blocks = projected.reshape(seq_rows, -1, GROUP + 2, HEAD)
    turning = head_blocks[:, :, : GROUP + 1, :]
    first_half = turning[..., : HEAD // 2]
    second_half = turning[..., HEAD // 2 :]
    cosine_wide = cosine_table[:, None, None, :]
    sine_wide = sine_table[:, None, None, :]
    turned = jnp.concatenate(
        [
            first_half * cosine_wide - second_half * sine_wide,
            second_half * cosine_wide + first_half * sine_wide,
        ],
        axis=-1,
    )
    head_blocks = jnp.concatenate([turned, head_blocks[:, :, GROUP + 1 :, :]], axis=2)
    return head_blocks.reshape(seq_rows, -1)


def normalize(embedded, norm_gain):
    values = embedded.astype(jnp.float32)
    mean_square = jnp.mean(values * values, axis=-1, keepdims=True)
    return (values * lax.rsqrt(mean_square + 1e-05) * norm_gain[None, :]).astype(jnp.bfloat16)


def gather_features(rows, tp_count):
    copies = jnp.broadcast_to(rows[None], (tp_count,) + rows.shape)
    blocks = lax.all_to_all(copies, "tp", 0, 0, tiled=True)
    return blocks.transpose(1, 0, 2).reshape(rows.shape[0], -1)


def shards(
    vit_context,
    vision_residual,
    out_weight,
    layer_scale,
    prompt,
    prompt_len,
    image_at,
    grid_sizes,
    image_owner,
    norm_gain,
    qkv_weight,
):
    requests = lax.axis_size(REQ)
    device_index = lax.axis_index(REQ)
    feature_width = vit_context.shape[1]
    merged_context = jnp.mean(
        vit_context.astype(jnp.float32).reshape(-1, 4, feature_width), axis=1
    ).astype(jnp.bfloat16)
    merged_residual = jnp.mean(
        vision_residual.astype(jnp.float32).reshape(-1, 4, feature_width), axis=1
    )
    full_prompt = gather_features(prompt[0], lax.axis_size("tp"))
    full_prompt, merged_context = lax.optimization_barrier((full_prompt, merged_context))
    core = lax.axis_index("rc")
    own_half = lax.all_gather(out_weight, "rxy", axis=1, tiled=True)
    other_half = lax.ppermute(own_half, "rc", [(0, 1), (1, 0)])
    own_part = jnp.dot(merged_context, own_half, preferred_element_type=jnp.float32)
    other_part = jnp.dot(merged_context, other_half, preferred_element_type=jnp.float32)
    own_part = own_part.reshape(own_part.shape[0], -1, 1, out_weight.shape[1])
    other_part = other_part.reshape(own_part.shape)
    partial_value = jnp.concatenate(
        [jnp.where(core == 0, own_part, other_part), jnp.where(core == 0, other_part, own_part)],
        axis=2,
    ).reshape(own_part.shape[0], -1)
    tp_count = lax.axis_size("tp")
    block_terms = partial_value.astype(jnp.bfloat16).reshape(
        -1, tp_count, feature_width
    ).transpose(1, 0, 2)
    own_share = jnp.sum(
        lax.all_to_all(block_terms, "tp", 0, 0, tiled=True).astype(jnp.float32), axis=0
    )
    merged = (merged_residual + layer_scale[None, :] * own_share).astype(jnp.bfloat16)
    merged_count = merged.shape[0]
    counts, starts = request_plan(grid_sizes, image_owner, requests)
    request_ends = starts + counts
    capacity = (IMG_MAX + requests - 1) // requests
    request_ids = jnp.arange(requests, dtype=jnp.int32)
    group_index = jnp.arange(merged_count, dtype=jnp.int32) * requests + device_index
    destination = jnp.sum((request_ends[None, :] <= group_index[:, None]).astype(jnp.int32), axis=1)
    owned_start = jnp.sum(
        jnp.where(destination[:, None] == request_ids[None, :], starts[None, :], 0), axis=1
    )
    target = destination * capacity + (group_index - owned_start) // requests
    usable = destination < requests
    send_slots = jnp.arange(requests * capacity, dtype=jnp.int32)
    placing = ((send_slots[:, None] == target[None, :]) & usable[None, :]).astype(jnp.bfloat16)
    outgoing = jnp.dot(placing, merged, preferred_element_type=jnp.float32).astype(jnp.bfloat16)
    arrived = lax.all_to_all(
        outgoing.reshape(requests, capacity, feature_width),
        REQ,
        split_axis=0,
        concat_axis=0,
        tiled=True,
    )
    arrived = arrived.reshape(requests * capacity, feature_width)
    own_request = request_ids == device_index
    own_count = jnp.sum(jnp.where(own_request, counts, 0))
    own_start = jnp.sum(jnp.where(own_request, starts, 0))
    image_from = image_at[0]
    prompt_count = prompt_len[0]
    seq_slots = prompt.shape[1] + IMG_MAX
    slot_index = jnp.arange(seq_slots, dtype=jnp.int32)
    image_row = slot_index - image_from
    in_image = (image_row >= 0) & (image_row < own_count)
    is_live = slot_index < prompt_count + own_count
    from_prompt = is_live & jnp.logical_not(in_image)
    flat_index = (own_start + image_row) % requests * capacity + image_row // requests
    image_pick = ((flat_index[:, None] == send_slots[None, :]) & in_image[:, None]).astype(
        jnp.bfloat16
    )
    prompt_row = jnp.where(slot_index < image_from, slot_index, slot_index - own_count)
    prompt_ids = jnp.arange(prompt.shape[1], dtype=jnp.int32)
    prompt_pick = ((prompt_row[:, None] == prompt_ids[None, :]) & from_prompt[:, None]).astype(
        jnp.bfloat16
    )
    full_image = gather_features(arrived, tp_count)
    embedded = (
        jnp.dot(image_pick, full_image, preferred_element_type=jnp.float32)
        + jnp.dot(prompt_pick, full_prompt, preferred_element_type=jnp.float32)
    ).astype(jnp.bfloat16)
    full_weight = lax.all_gather(qkv_weight, REQ, axis=0, tiled=True)
    normed = normalize(embedded, norm_gain)
    projected = jnp.dot(normed, full_weight, preferred_element_type=jnp.float32)
    cosine_table, sine_table = rope_tables(seq_slots)
    return apply_rope(projected, cosine_table, sine_table).astype(jnp.bfloat16)


def solution(mesh):
    in_specs = (
        P("req", "tp"),
        P("req", "tp"),
        P("tp", "req"),
        P("tp"),
        P("req", None, "tp"),
        P("req"),
        P("req"),
        P(),
        P(),
        P(),
        P("req", "tp"),
    )
    out_specs = P("req", "tp")
    rows, columns = mesh.devices.shape
    split_mesh = Mesh(mesh.devices.reshape(rows // 2, 2, columns), ("rxy", "rc", "tp"))
    rename = lambda spec: P(*(REQ if axis == "req" else axis for axis in spec))
    return jax.shard_map(
        shards,
        mesh=split_mesh,
        in_specs=tuple(rename(spec) for spec in in_specs),
        out_specs=rename(out_specs),
        check_vma=False,
    )
```

```python
import jax
import jax.numpy as jnp
from jax import lax
from jax.sharding import Mesh, PartitionSpec as P

HEAD = 128
GROUP = 4
IMG_MAX = 128
REQ = ("rx", "ry", "rc")


def request_plan(grid_sizes, image_owner, requests):
    image_rows = grid_sizes[:, 0] * grid_sizes[:, 1]
    member = (image_owner[:, None] == jnp.arange(requests, dtype=jnp.int32)[None, :]).astype(
        jnp.int32
    )
    counts = jnp.sum(image_rows[:, None] * member, axis=0)
    starts = jnp.cumsum(counts) - counts
    return (counts, starts)


def rope_tables(count):
    half_size = HEAD // 2
    exponent = jnp.arange(half_size, dtype=jnp.float32) * (2.0 / HEAD)
    frequency = jnp.exp(-exponent * jnp.log(jnp.float32(500000.0)))
    angles = jnp.arange(count, dtype=jnp.float32)[:, None] * frequency[None, :]
    return (jnp.cos(angles), jnp.sin(angles))


def apply_rope(projected, cosine_table, sine_table):
    seq_rows = projected.shape[0]
    head_blocks = projected.reshape(seq_rows, -1, GROUP + 2, HEAD)
    turning = head_blocks[:, :, : GROUP + 1, :]
    first_half = turning[..., : HEAD // 2]
    second_half = turning[..., HEAD // 2 :]
    cosine_wide = cosine_table[:, None, None, :]
    sine_wide = sine_table[:, None, None, :]
    turned = jnp.concatenate(
        [
            first_half * cosine_wide - second_half * sine_wide,
            second_half * cosine_wide + first_half * sine_wide,
        ],
        axis=-1,
    )
    head_blocks = jnp.concatenate([turned, head_blocks[:, :, GROUP + 1 :, :]], axis=2)
    return head_blocks.reshape(seq_rows, -1)


def normalize(embedded, norm_gain):
    values = embedded.astype(jnp.float32)
    mean_square = jnp.mean(values * values, axis=-1, keepdims=True)
    return (values * lax.rsqrt(mean_square + 1e-05) * norm_gain[None, :]).astype(jnp.bfloat16)


def gather_features(rows, tp_count):
    copies = jnp.broadcast_to(rows[None], (tp_count,) + rows.shape)
    blocks = lax.all_to_all(copies, "tp", 0, 0, tiled=True)
    return blocks.transpose(1, 0, 2).reshape(rows.shape[0], -1)


def shift(value, axis, step):
    size = lax.axis_size(axis)
    return lax.ppermute(value, axis, [(k, (k + step) % size) for k in range(size)])


def ring_gather(value, axis):
    size = lax.axis_size(axis)
    forward, backward = value, value
    after = {}
    for step in range(1, size // 2 + 1):
        if step == size // 2 and size % 2 == 0:
            half = value.shape[-1] // 2
            left = shift(forward[..., :half], axis, 1)
            right = shift(backward[..., half:], axis, -1)
            after[step] = jnp.concatenate([left, right], axis=-1)
            break
        forward = shift(forward, axis, 1)
        backward = shift(backward, axis, -1)
        after[size - step] = forward
        after[step] = backward
    relative = jnp.stack([value] + [after[step] for step in range(1, size)], axis=0)
    return jnp.roll(relative, lax.axis_index(axis), axis=0)


def gather_plane(shard):
    by_y = ring_gather(shard, "ry")
    return ring_gather(by_y, "rx")


def shards(
    vit_context,
    vision_residual,
    out_weight,
    layer_scale,
    prompt,
    prompt_len,
    image_at,
    grid_sizes,
    image_owner,
    norm_gain,
    qkv_weight,
):
    requests = lax.axis_size(REQ)
    device_index = lax.axis_index(REQ)
    feature_width = vit_context.shape[1]
    merged_context = jnp.mean(
        vit_context.astype(jnp.float32).reshape(-1, 4, feature_width), axis=1
    ).astype(jnp.bfloat16)
    merged_residual = jnp.mean(
        vision_residual.astype(jnp.float32).reshape(-1, 4, feature_width), axis=1
    )
    own_half = gather_plane(out_weight)
    other_half = lax.ppermute(own_half, "rc", [(0, 1), (1, 0)])
    core = lax.axis_index("rc")
    own_part = jnp.einsum(
        "gk,xykn->gxyn", merged_context, own_half, preferred_element_type=jnp.float32
    )
    other_part = jnp.einsum(
        "gk,xykn->gxyn", merged_context, other_half, preferred_element_type=jnp.float32
    )
    partial_value = jnp.stack(
        [jnp.where(core == 0, own_part, other_part), jnp.where(core == 0, other_part, own_part)],
        axis=3,
    ).reshape(own_part.shape[0], -1)
    tp_count = lax.axis_size("tp")
    full_prompt = gather_features(prompt[0], tp_count)
    full_prompt, partial_value = lax.optimization_barrier((full_prompt, partial_value))
    block_terms = partial_value.astype(jnp.bfloat16).reshape(
        -1, tp_count, feature_width
    ).transpose(1, 0, 2)
    own_share = jnp.sum(
        lax.all_to_all(block_terms, "tp", 0, 0, tiled=True).astype(jnp.float32), axis=0
    )
    merged = (merged_residual + layer_scale[None, :] * own_share).astype(jnp.bfloat16)
    merged_count = merged.shape[0]
    counts, starts = request_plan(grid_sizes, image_owner, requests)
    request_ends = starts + counts
    capacity = (IMG_MAX + requests - 1) // requests
    request_ids = jnp.arange(requests, dtype=jnp.int32)
    group_index = jnp.arange(merged_count, dtype=jnp.int32) * requests + device_index
    destination = jnp.sum((request_ends[None, :] <= group_index[:, None]).astype(jnp.int32), axis=1)
    owned_start = jnp.sum(
        jnp.where(destination[:, None] == request_ids[None, :], starts[None, :], 0), axis=1
    )
    target = destination * capacity + (group_index - owned_start) // requests
    usable = destination < requests
    send_slots = jnp.arange(requests * capacity, dtype=jnp.int32)
    placing = ((send_slots[:, None] == target[None, :]) & usable[None, :]).astype(jnp.bfloat16)
    outgoing = jnp.dot(placing, merged, preferred_element_type=jnp.float32).astype(jnp.bfloat16)
    arrived = lax.all_to_all(
        outgoing.reshape(requests, capacity, feature_width),
        REQ,
        split_axis=0,
        concat_axis=0,
        tiled=True,
    )
    arrived = arrived.reshape(requests * capacity, feature_width)
    own_request = request_ids == device_index
    own_count = jnp.sum(jnp.where(own_request, counts, 0))
    own_start = jnp.sum(jnp.where(own_request, starts, 0))
    image_from = image_at[0]
    prompt_count = prompt_len[0]
    seq_slots = prompt.shape[1] + IMG_MAX
    slot_index = jnp.arange(seq_slots, dtype=jnp.int32)
    image_row = slot_index - image_from
    in_image = (image_row >= 0) & (image_row < own_count)
    is_live = slot_index < prompt_count + own_count
    from_prompt = is_live & jnp.logical_not(in_image)
    flat_index = (own_start + image_row) % requests * capacity + image_row // requests
    image_pick = ((flat_index[:, None] == send_slots[None, :]) & in_image[:, None]).astype(
        jnp.bfloat16
    )
    prompt_row = jnp.where(slot_index < image_from, slot_index, slot_index - own_count)
    prompt_ids = jnp.arange(prompt.shape[1], dtype=jnp.int32)
    prompt_pick = ((prompt_row[:, None] == prompt_ids[None, :]) & from_prompt[:, None]).astype(
        jnp.bfloat16
    )
    full_image = gather_features(arrived, tp_count)
    embedded = (
        jnp.dot(image_pick, full_image, preferred_element_type=jnp.float32)
        + jnp.dot(prompt_pick, full_prompt, preferred_element_type=jnp.float32)
    ).astype(jnp.bfloat16)
    full_weight = lax.all_gather(qkv_weight, REQ, axis=0, tiled=True)
    normed = normalize(embedded, norm_gain)
    projected = jnp.dot(normed, full_weight, preferred_element_type=jnp.float32)
    cosine_table, sine_table = rope_tables(seq_slots)
    return apply_rope(projected, cosine_table, sine_table).astype(jnp.bfloat16)


def solution(mesh):
    in_specs = (
        P("req", "tp"),
        P("req", "tp"),
        P("tp", "req"),
        P("tp"),
        P("req", None, "tp"),
        P("req"),
        P("req"),
        P(),
        P(),
        P(),
        P("req", "tp"),
    )
    out_specs = P("req", "tp")
    rows, columns = mesh.devices.shape
    x_size = len({device.coords[0] for device in mesh.devices.flat})
    split_mesh = Mesh(
        mesh.devices.reshape(x_size, rows // (2 * x_size), 2, columns), REQ + ("tp",)
    )
    rename = lambda spec: P(*(REQ if axis == "req" else axis for axis in spec))
    return jax.shard_map(
        shards,
        mesh=split_mesh,
        in_specs=tuple(rename(spec) for spec in in_specs),
        out_specs=rename(out_specs),
        check_vma=False,
    )
```

```python
import jax
import jax.numpy as jnp
from jax import lax
from jax.sharding import PartitionSpec as P

HEAD = 128
GROUP = 4
IMG_MAX = 128


def request_plan(grid_sizes, image_owner, requests):
    image_rows = grid_sizes[:, 0] * grid_sizes[:, 1]
    member = (image_owner[:, None] == jnp.arange(requests, dtype=jnp.int32)[None, :]).astype(
        jnp.int32
    )
    counts = jnp.sum(image_rows[:, None] * member, axis=0)
    starts = jnp.cumsum(counts) - counts
    return (counts, starts)


def rope_tables(count):
    half_size = HEAD // 2
    exponent = jnp.arange(half_size, dtype=jnp.float32) * (2.0 / HEAD)
    frequency = jnp.exp(-exponent * jnp.log(jnp.float32(500000.0)))
    angles = jnp.arange(count, dtype=jnp.float32)[:, None] * frequency[None, :]
    return (jnp.cos(angles), jnp.sin(angles))


def apply_rope(projected, cosine_table, sine_table):
    seq_rows = projected.shape[0]
    head_blocks = projected.reshape(seq_rows, -1, GROUP + 2, HEAD)
    turning = head_blocks[:, :, : GROUP + 1, :]
    first_half = turning[..., : HEAD // 2]
    second_half = turning[..., HEAD // 2 :]
    cosine_wide = cosine_table[:, None, None, :]
    sine_wide = sine_table[:, None, None, :]
    turned = jnp.concatenate(
        [
            first_half * cosine_wide - second_half * sine_wide,
            second_half * cosine_wide + first_half * sine_wide,
        ],
        axis=-1,
    )
    head_blocks = jnp.concatenate([turned, head_blocks[:, :, GROUP + 1 :, :]], axis=2)
    return head_blocks.reshape(seq_rows, -1)


def normalize(embedded, norm_gain):
    values = embedded.astype(jnp.float32)
    mean_square = jnp.mean(values * values, axis=-1, keepdims=True)
    return (values * lax.rsqrt(mean_square + 1e-05) * norm_gain[None, :]).astype(jnp.bfloat16)


def gather_features(rows, tp_count):
    copies = jnp.broadcast_to(rows[None], (tp_count,) + rows.shape)
    blocks = lax.all_to_all(copies, "tp", 0, 0, tiled=True)
    return blocks.transpose(1, 0, 2).reshape(rows.shape[0], -1)


def shards(
    vit_context,
    vision_residual,
    out_weight,
    layer_scale,
    prompt,
    prompt_len,
    image_at,
    grid_sizes,
    image_owner,
    norm_gain,
    qkv_weight,
):
    requests = lax.axis_size("req")
    device_index = lax.axis_index("req")
    feature_width = vit_context.shape[1]
    merged_context = jnp.mean(
        vit_context.astype(jnp.float32).reshape(-1, 4, feature_width), axis=1
    ).astype(jnp.bfloat16)
    merged_residual = jnp.mean(
        vision_residual.astype(jnp.float32).reshape(-1, 4, feature_width), axis=1
    )
    full_prompt = gather_features(prompt[0], lax.axis_size("tp"))
    full_prompt, merged_context = lax.optimization_barrier((full_prompt, merged_context))
    partial_value = jnp.dot(
        merged_context,
        lax.all_gather(out_weight, "req", axis=1, tiled=True),
        preferred_element_type=jnp.float32,
    )
    tp_count = lax.axis_size("tp")
    merged_count = merged_context.shape[0]
    counts, starts = request_plan(grid_sizes, image_owner, requests)
    request_ends = starts + counts
    capacity = (IMG_MAX + requests - 1) // requests
    request_ids = jnp.arange(requests, dtype=jnp.int32)
    group_index = jnp.arange(merged_count, dtype=jnp.int32) * requests + device_index
    destination = jnp.sum((request_ends[None, :] <= group_index[:, None]).astype(jnp.int32), axis=1)
    owned_start = jnp.sum(
        jnp.where(destination[:, None] == request_ids[None, :], starts[None, :], 0), axis=1
    )
    target = destination * capacity + (group_index - owned_start) // requests
    usable = destination < requests
    send_slots = jnp.arange(requests * capacity, dtype=jnp.int32)
    sends = (send_slots[:, None] == target[None, :]) & usable[None, :]
    slot_used = jnp.any(sends, axis=1)
    source_group = jnp.sum(jnp.where(sends, jnp.arange(merged_count)[None, :], 0), axis=1)
    residual_out = jnp.where(slot_used[:, None], merged_residual[source_group], 0.0)
    residual_in = lax.all_to_all(
        residual_out.reshape(requests, capacity, feature_width), "req", 0, 0, tiled=True
    ).reshape(requests * capacity, feature_width)
    terms = partial_value.astype(jnp.bfloat16)
    terms_out = jnp.where(slot_used[:, None], terms[source_group], jnp.zeros_like(terms[:1]))
    terms_out = terms_out.reshape(requests, capacity, tp_count, feature_width).transpose(0, 2, 1, 3)
    terms_in = lax.all_to_all(
        terms_out.reshape(requests * tp_count, capacity, feature_width),
        ("req", "tp"),
        0,
        0,
        tiled=True,
    ).reshape(requests, tp_count, capacity, feature_width)
    image_sum = jnp.sum(terms_in.astype(jnp.float32), axis=1).reshape(-1, feature_width)
    arrived = (residual_in + layer_scale[None, :] * image_sum).astype(jnp.bfloat16)
    own_request = request_ids == device_index
    own_count = jnp.sum(jnp.where(own_request, counts, 0))
    own_start = jnp.sum(jnp.where(own_request, starts, 0))
    image_from = image_at[0]
    prompt_count = prompt_len[0]
    seq_slots = prompt.shape[1] + IMG_MAX
    slot_index = jnp.arange(seq_slots, dtype=jnp.int32)
    image_row = slot_index - image_from
    in_image = (image_row >= 0) & (image_row < own_count)
    is_live = slot_index < prompt_count + own_count
    from_prompt = is_live & jnp.logical_not(in_image)
    flat_index = (own_start + image_row) % requests * capacity + image_row // requests
    image_pick = ((flat_index[:, None] == send_slots[None, :]) & in_image[:, None]).astype(
        jnp.bfloat16
    )
    prompt_row = jnp.where(slot_index < image_from, slot_index, slot_index - own_count)
    prompt_ids = jnp.arange(prompt.shape[1], dtype=jnp.int32)
    prompt_pick = ((prompt_row[:, None] == prompt_ids[None, :]) & from_prompt[:, None]).astype(
        jnp.bfloat16
    )
    full_image = gather_features(arrived, tp_count)
    embedded = (
        jnp.dot(image_pick, full_image, preferred_element_type=jnp.float32)
        + jnp.dot(prompt_pick, full_prompt, preferred_element_type=jnp.float32)
    ).astype(jnp.bfloat16)
    full_weight = lax.all_gather(qkv_weight, "req", axis=0, tiled=True)
    normed = normalize(embedded, norm_gain)
    projected = jnp.dot(normed, full_weight, preferred_element_type=jnp.float32)
    cosine_table, sine_table = rope_tables(seq_slots)
    return apply_rope(projected, cosine_table, sine_table).astype(jnp.bfloat16)


def solution(mesh):
    in_specs = (
        P("req", "tp"),
        P("req", "tp"),
        P("tp", "req"),
        P("tp"),
        P("req", None, "tp"),
        P("req"),
        P("req"),
        P(),
        P(),
        P(),
        P("req", "tp"),
    )
    out_specs = P("req", "tp")
    return jax.shard_map(shards, mesh=mesh, in_specs=in_specs, out_specs=out_specs, check_vma=False)
```

```python
import jax
import jax.numpy as jnp
from jax import lax
from jax.sharding import Mesh, PartitionSpec as P

HEAD = 128
GROUP = 4
IMG_MAX = 128
REQ = ("rx", "ry", "rc")


def request_plan(grid_sizes, image_owner, requests):
    image_rows = grid_sizes[:, 0] * grid_sizes[:, 1]
    member = (image_owner[:, None] == jnp.arange(requests, dtype=jnp.int32)[None, :]).astype(
        jnp.int32
    )
    counts = jnp.sum(image_rows[:, None] * member, axis=0)
    starts = jnp.cumsum(counts) - counts
    return (counts, starts)


def rope_tables(count):
    half_size = HEAD // 2
    exponent = jnp.arange(half_size, dtype=jnp.float32) * (2.0 / HEAD)
    frequency = jnp.exp(-exponent * jnp.log(jnp.float32(500000.0)))
    angles = jnp.arange(count, dtype=jnp.float32)[:, None] * frequency[None, :]
    return (jnp.cos(angles), jnp.sin(angles))


def apply_rope(projected, cosine_table, sine_table):
    seq_rows = projected.shape[0]
    head_blocks = projected.reshape(seq_rows, -1, GROUP + 2, HEAD)
    turning = head_blocks[:, :, : GROUP + 1, :]
    first_half = turning[..., : HEAD // 2]
    second_half = turning[..., HEAD // 2 :]
    cosine_wide = cosine_table[:, None, None, :]
    sine_wide = sine_table[:, None, None, :]
    turned = jnp.concatenate(
        [
            first_half * cosine_wide - second_half * sine_wide,
            second_half * cosine_wide + first_half * sine_wide,
        ],
        axis=-1,
    )
    head_blocks = jnp.concatenate([turned, head_blocks[:, :, GROUP + 1 :, :]], axis=2)
    return head_blocks.reshape(seq_rows, -1)


def normalize(embedded, norm_gain):
    values = embedded.astype(jnp.float32)
    mean_square = jnp.mean(values * values, axis=-1, keepdims=True)
    return (values * lax.rsqrt(mean_square + 1e-05) * norm_gain[None, :]).astype(jnp.bfloat16)


def gather_features(rows, tp_count):
    copies = jnp.broadcast_to(rows[None], (tp_count,) + rows.shape)
    blocks = lax.all_to_all(copies, "tp", 0, 0, tiled=True)
    return blocks.transpose(1, 0, 2).reshape(rows.shape[0], -1)


def shift(value, axis, step):
    size = lax.axis_size(axis)
    return lax.ppermute(value, axis, [(k, (k + step) % size) for k in range(size)])


def ring_gather(value, axis):
    size = lax.axis_size(axis)
    forward, backward = value, value
    after = {}
    for step in range(1, size // 2 + 1):
        if step == size // 2 and size % 2 == 0:
            half = value.shape[-1] // 2
            left = shift(forward[..., :half], axis, 1)
            right = shift(backward[..., half:], axis, -1)
            after[step] = jnp.concatenate([left, right], axis=-1)
            break
        forward = shift(forward, axis, 1)
        backward = shift(backward, axis, -1)
        after[size - step] = forward
        after[step] = backward
    relative = jnp.stack([value] + [after[step] for step in range(1, size)], axis=0)
    return jnp.roll(relative, lax.axis_index(axis), axis=0)


def gather_plane(shard):
    by_y = ring_gather(shard, "ry")
    return ring_gather(by_y, "rx")


def shards(
    vit_context,
    vision_residual,
    out_weight,
    layer_scale,
    prompt,
    prompt_len,
    image_at,
    grid_sizes,
    image_owner,
    norm_gain,
    qkv_weight,
):
    requests = lax.axis_size(REQ)
    device_index = lax.axis_index(REQ)
    feature_width = vit_context.shape[1]
    merged_context = jnp.mean(
        vit_context.astype(jnp.float32).reshape(-1, 4, feature_width), axis=1
    ).astype(jnp.bfloat16)
    merged_residual = jnp.mean(
        vision_residual.astype(jnp.float32).reshape(-1, 4, feature_width), axis=1
    )
    own_half = gather_plane(out_weight)
    other_half = lax.ppermute(own_half, "rc", [(0, 1), (1, 0)])
    core = lax.axis_index("rc")
    own_part = jnp.einsum(
        "gk,xykn->gxyn", merged_context, own_half, preferred_element_type=jnp.float32
    )
    other_part = jnp.einsum(
        "gk,xykn->gxyn", merged_context, other_half, preferred_element_type=jnp.float32
    )
    partial_value = jnp.stack(
        [jnp.where(core == 0, own_part, other_part), jnp.where(core == 0, other_part, own_part)],
        axis=3,
    ).reshape(own_part.shape[0], -1)
    tp_count = lax.axis_size("tp")
    block_terms = partial_value.astype(jnp.bfloat16).reshape(
        -1, tp_count, feature_width
    ).transpose(1, 0, 2)
    own_share = jnp.sum(
        lax.all_to_all(block_terms, "tp", 0, 0, tiled=True).astype(jnp.float32), axis=0
    )
    merged = (merged_residual + layer_scale[None, :] * own_share).astype(jnp.bfloat16)
    merged_count = merged.shape[0]
    counts, starts = request_plan(grid_sizes, image_owner, requests)
    request_ends = starts + counts
    capacity = (IMG_MAX + requests - 1) // requests
    request_ids = jnp.arange(requests, dtype=jnp.int32)
    group_index = jnp.arange(merged_count, dtype=jnp.int32) * requests + device_index
    destination = jnp.sum((request_ends[None, :] <= group_index[:, None]).astype(jnp.int32), axis=1)
    owned_start = jnp.sum(
        jnp.where(destination[:, None] == request_ids[None, :], starts[None, :], 0), axis=1
    )
    target = destination * capacity + (group_index - owned_start) // requests
    usable = destination < requests
    send_slots = jnp.arange(requests * capacity, dtype=jnp.int32)
    placing = ((send_slots[:, None] == target[None, :]) & usable[None, :]).astype(jnp.bfloat16)
    outgoing = jnp.dot(placing, merged, preferred_element_type=jnp.float32).astype(jnp.bfloat16)
    arrived = lax.all_to_all(
        outgoing.reshape(requests, capacity, feature_width),
        REQ,
        split_axis=0,
        concat_axis=0,
        tiled=True,
    )
    arrived = arrived.reshape(requests * capacity, feature_width)
    own_request = request_ids == device_index
    own_count = jnp.sum(jnp.where(own_request, counts, 0))
    own_start = jnp.sum(jnp.where(own_request, starts, 0))
    image_from = image_at[0]
    prompt_count = prompt_len[0]
    seq_slots = prompt.shape[1] + IMG_MAX
    slot_index = jnp.arange(seq_slots, dtype=jnp.int32)
    image_row = slot_index - image_from
    in_image = (image_row >= 0) & (image_row < own_count)
    is_live = slot_index < prompt_count + own_count
    from_prompt = is_live & jnp.logical_not(in_image)
    flat_index = (own_start + image_row) % requests * capacity + image_row // requests
    image_pick = ((flat_index[:, None] == send_slots[None, :]) & in_image[:, None]).astype(
        jnp.bfloat16
    )
    prompt_row = jnp.where(slot_index < image_from, slot_index, slot_index - own_count)
    prompt_ids = jnp.arange(prompt.shape[1], dtype=jnp.int32)
    prompt_pick = ((prompt_row[:, None] == prompt_ids[None, :]) & from_prompt[:, None]).astype(
        jnp.bfloat16
    )
    full_image = gather_features(arrived, tp_count)
    full_prompt = lax.all_gather(prompt[0], "tp", axis=1, tiled=True)
    embedded = (
        jnp.dot(image_pick, full_image, preferred_element_type=jnp.float32)
        + jnp.dot(prompt_pick, full_prompt, preferred_element_type=jnp.float32)
    ).astype(jnp.bfloat16)
    full_weight = lax.all_gather(qkv_weight, REQ, axis=0, tiled=True)
    normed = normalize(embedded, norm_gain)
    projected = jnp.dot(normed, full_weight, preferred_element_type=jnp.float32)
    cosine_table, sine_table = rope_tables(seq_slots)
    return apply_rope(projected, cosine_table, sine_table).astype(jnp.bfloat16)


def solution(mesh):
    in_specs = (
        P("req", "tp"),
        P("req", "tp"),
        P("tp", "req"),
        P("tp"),
        P("req", None, "tp"),
        P("req"),
        P("req"),
        P(),
        P(),
        P(),
        P("req", "tp"),
    )
    out_specs = P("req", "tp")
    rows, columns = mesh.devices.shape
    x_size = len({device.coords[0] for device in mesh.devices.flat})
    split_mesh = Mesh(
        mesh.devices.reshape(x_size, rows // (2 * x_size), 2, columns), REQ + ("tp",)
    )
    rename = lambda spec: P(*(REQ if axis == "req" else axis for axis in spec))
    return jax.shard_map(
        shards,
        mesh=split_mesh,
        in_specs=tuple(rename(spec) for spec in in_specs),
        out_specs=rename(out_specs),
        check_vma=False,
    )
```

```python
import jax
import jax.numpy as jnp
from jax import lax
from jax.sharding import Mesh, PartitionSpec as P

HEAD = 128
GROUP = 4
IMG_MAX = 128
REQ = ("rx", "ry", "rc")


def request_plan(grid_sizes, image_owner, requests):
    image_rows = grid_sizes[:, 0] * grid_sizes[:, 1]
    member = (image_owner[:, None] == jnp.arange(requests, dtype=jnp.int32)[None, :]).astype(
        jnp.int32
    )
    counts = jnp.sum(image_rows[:, None] * member, axis=0)
    starts = jnp.cumsum(counts) - counts
    return (counts, starts)


def rope_tables(count):
    half_size = HEAD // 2
    exponent = jnp.arange(half_size, dtype=jnp.float32) * (2.0 / HEAD)
    frequency = jnp.exp(-exponent * jnp.log(jnp.float32(500000.0)))
    angles = jnp.arange(count, dtype=jnp.float32)[:, None] * frequency[None, :]
    return (jnp.cos(angles), jnp.sin(angles))


def apply_rope(projected, cosine_table, sine_table):
    seq_rows = projected.shape[0]
    head_blocks = projected.reshape(seq_rows, -1, GROUP + 2, HEAD)
    turning = head_blocks[:, :, : GROUP + 1, :]
    first_half = turning[..., : HEAD // 2]
    second_half = turning[..., HEAD // 2 :]
    cosine_wide = cosine_table[:, None, None, :]
    sine_wide = sine_table[:, None, None, :]
    turned = jnp.concatenate(
        [
            first_half * cosine_wide - second_half * sine_wide,
            second_half * cosine_wide + first_half * sine_wide,
        ],
        axis=-1,
    )
    head_blocks = jnp.concatenate([turned, head_blocks[:, :, GROUP + 1 :, :]], axis=2)
    return head_blocks.reshape(seq_rows, -1)


def normalize(embedded, norm_gain):
    values = embedded.astype(jnp.float32)
    mean_square = jnp.mean(values * values, axis=-1, keepdims=True)
    return (values * lax.rsqrt(mean_square + 1e-05) * norm_gain[None, :]).astype(jnp.bfloat16)


def gather_features(rows, tp_count):
    copies = jnp.broadcast_to(rows[None], (tp_count,) + rows.shape)
    blocks = lax.all_to_all(copies, "tp", 0, 0, tiled=True)
    return blocks.transpose(1, 0, 2).reshape(rows.shape[0], -1)


def shift(value, axis, step):
    size = lax.axis_size(axis)
    return lax.ppermute(value, axis, [(k, (k + step) % size) for k in range(size)])


def ring_gather(value, axis):
    size = lax.axis_size(axis)
    relative = jnp.stack([value] + [shift(value, axis, -step) for step in range(1, size)], axis=0)
    return jnp.roll(relative, lax.axis_index(axis), axis=0)


def gather_plane(shard):
    by_y = ring_gather(shard, "ry")
    return ring_gather(by_y, "rx")


def shards(
    vit_context,
    vision_residual,
    out_weight,
    layer_scale,
    prompt,
    prompt_len,
    image_at,
    grid_sizes,
    image_owner,
    norm_gain,
    qkv_weight,
):
    requests = lax.axis_size(REQ)
    device_index = lax.axis_index(REQ)
    feature_width = vit_context.shape[1]
    merged_context = jnp.mean(
        vit_context.astype(jnp.float32).reshape(-1, 4, feature_width), axis=1
    ).astype(jnp.bfloat16)
    merged_residual = jnp.mean(
        vision_residual.astype(jnp.float32).reshape(-1, 4, feature_width), axis=1
    )
    own_half = gather_plane(out_weight)
    other_half = lax.ppermute(own_half, "rc", [(0, 1), (1, 0)])
    core = lax.axis_index("rc")
    own_part = jnp.einsum(
        "gk,xykn->gxyn", merged_context, own_half, preferred_element_type=jnp.float32
    )
    other_part = jnp.einsum(
        "gk,xykn->gxyn", merged_context, other_half, preferred_element_type=jnp.float32
    )
    partial_value = jnp.stack(
        [jnp.where(core == 0, own_part, other_part), jnp.where(core == 0, other_part, own_part)],
        axis=3,
    ).reshape(own_part.shape[0], -1)
    tp_count = lax.axis_size("tp")
    block_terms = partial_value.astype(jnp.bfloat16).reshape(
        -1, tp_count, feature_width
    ).transpose(1, 0, 2)
    own_share = jnp.sum(
        lax.all_to_all(block_terms, "tp", 0, 0, tiled=True).astype(jnp.float32), axis=0
    )
    merged = (merged_residual + layer_scale[None, :] * own_share).astype(jnp.bfloat16)
    merged_count = merged.shape[0]
    counts, starts = request_plan(grid_sizes, image_owner, requests)
    request_ends = starts + counts
    capacity = (IMG_MAX + requests - 1) // requests
    request_ids = jnp.arange(requests, dtype=jnp.int32)
    group_index = jnp.arange(merged_count, dtype=jnp.int32) * requests + device_index
    destination = jnp.sum((request_ends[None, :] <= group_index[:, None]).astype(jnp.int32), axis=1)
    owned_start = jnp.sum(
        jnp.where(destination[:, None] == request_ids[None, :], starts[None, :], 0), axis=1
    )
    target = destination * capacity + (group_index - owned_start) // requests
    usable = destination < requests
    send_slots = jnp.arange(requests * capacity, dtype=jnp.int32)
    placing = ((send_slots[:, None] == target[None, :]) & usable[None, :]).astype(jnp.bfloat16)
    outgoing = jnp.dot(placing, merged, preferred_element_type=jnp.float32).astype(jnp.bfloat16)
    arrived = lax.all_to_all(
        outgoing.reshape(requests, capacity, feature_width),
        REQ,
        split_axis=0,
        concat_axis=0,
        tiled=True,
    )
    arrived = arrived.reshape(requests * capacity, feature_width)
    own_request = request_ids == device_index
    own_count = jnp.sum(jnp.where(own_request, counts, 0))
    own_start = jnp.sum(jnp.where(own_request, starts, 0))
    image_from = image_at[0]
    prompt_count = prompt_len[0]
    seq_slots = prompt.shape[1] + IMG_MAX
    slot_index = jnp.arange(seq_slots, dtype=jnp.int32)
    image_row = slot_index - image_from
    in_image = (image_row >= 0) & (image_row < own_count)
    is_live = slot_index < prompt_count + own_count
    from_prompt = is_live & jnp.logical_not(in_image)
    flat_index = (own_start + image_row) % requests * capacity + image_row // requests
    image_pick = ((flat_index[:, None] == send_slots[None, :]) & in_image[:, None]).astype(
        jnp.bfloat16
    )
    prompt_row = jnp.where(slot_index < image_from, slot_index, slot_index - own_count)
    prompt_ids = jnp.arange(prompt.shape[1], dtype=jnp.int32)
    prompt_pick = ((prompt_row[:, None] == prompt_ids[None, :]) & from_prompt[:, None]).astype(
        jnp.bfloat16
    )
    full_image = gather_features(arrived, tp_count)
    full_prompt = lax.all_gather(prompt[0], "tp", axis=1, tiled=True)
    embedded = (
        jnp.dot(image_pick, full_image, preferred_element_type=jnp.float32)
        + jnp.dot(prompt_pick, full_prompt, preferred_element_type=jnp.float32)
    ).astype(jnp.bfloat16)
    full_weight = lax.all_gather(qkv_weight, REQ, axis=0, tiled=True)
    normed = normalize(embedded, norm_gain)
    projected = jnp.dot(normed, full_weight, preferred_element_type=jnp.float32)
    cosine_table, sine_table = rope_tables(seq_slots)
    return apply_rope(projected, cosine_table, sine_table).astype(jnp.bfloat16)


def solution(mesh):
    in_specs = (
        P("req", "tp"),
        P("req", "tp"),
        P("tp", "req"),
        P("tp"),
        P("req", None, "tp"),
        P("req"),
        P("req"),
        P(),
        P(),
        P(),
        P("req", "tp"),
    )
    out_specs = P("req", "tp")
    rows, columns = mesh.devices.shape
    x_size = len({device.coords[0] for device in mesh.devices.flat})
    split_mesh = Mesh(
        mesh.devices.reshape(x_size, rows // (2 * x_size), 2, columns), REQ + ("tp",)
    )
    rename = lambda spec: P(*(REQ if axis == "req" else axis for axis in spec))
    return jax.shard_map(
        shards,
        mesh=split_mesh,
        in_specs=tuple(rename(spec) for spec in in_specs),
        out_specs=rename(out_specs),
        check_vma=False,
    )
```

```python
import jax
import jax.numpy as jnp
from jax import lax
from jax.sharding import Mesh, PartitionSpec as P

HEAD = 128
GROUP = 4
IMG_MAX = 128
REQ = ("rx", "ry", "rc")


def request_plan(grid_sizes, image_owner, requests):
    image_rows = grid_sizes[:, 0] * grid_sizes[:, 1]
    member = (image_owner[:, None] == jnp.arange(requests, dtype=jnp.int32)[None, :]).astype(
        jnp.int32
    )
    counts = jnp.sum(image_rows[:, None] * member, axis=0)
    starts = jnp.cumsum(counts) - counts
    return (counts, starts)


def rope_tables(count):
    half_size = HEAD // 2
    exponent = jnp.arange(half_size, dtype=jnp.float32) * (2.0 / HEAD)
    frequency = jnp.exp(-exponent * jnp.log(jnp.float32(500000.0)))
    angles = jnp.arange(count, dtype=jnp.float32)[:, None] * frequency[None, :]
    return (jnp.cos(angles), jnp.sin(angles))


def apply_rope(projected, cosine_table, sine_table):
    seq_rows = projected.shape[0]
    head_blocks = projected.reshape(seq_rows, -1, GROUP + 2, HEAD)
    turning = head_blocks[:, :, : GROUP + 1, :]
    first_half = turning[..., : HEAD // 2]
    second_half = turning[..., HEAD // 2 :]
    cosine_wide = cosine_table[:, None, None, :]
    sine_wide = sine_table[:, None, None, :]
    turned = jnp.concatenate(
        [
            first_half * cosine_wide - second_half * sine_wide,
            second_half * cosine_wide + first_half * sine_wide,
        ],
        axis=-1,
    )
    head_blocks = jnp.concatenate([turned, head_blocks[:, :, GROUP + 1 :, :]], axis=2)
    return head_blocks.reshape(seq_rows, -1)


def normalize(embedded, norm_gain):
    values = embedded.astype(jnp.float32)
    mean_square = jnp.mean(values * values, axis=-1, keepdims=True)
    return (values * lax.rsqrt(mean_square + 1e-05) * norm_gain[None, :]).astype(jnp.bfloat16)


def gather_features(rows, tp_count):
    copies = jnp.broadcast_to(rows[None], (tp_count,) + rows.shape)
    blocks = lax.all_to_all(copies, "tp", 0, 0, tiled=True)
    return blocks.transpose(1, 0, 2).reshape(rows.shape[0], -1)


def shift(value, axis, step):
    size = lax.axis_size(axis)
    return lax.ppermute(value, axis, [(k, (k + step) % size) for k in range(size)])


def ring_gather(value, axis):
    size = lax.axis_size(axis)
    return jnp.stack([value] + [shift(value, axis, -step) for step in range(1, size)], axis=0)


def gather_plane(shard):
    by_y = ring_gather(shard, "ry")
    return ring_gather(by_y, "rx")


def shards(
    vit_context,
    vision_residual,
    out_weight,
    layer_scale,
    prompt,
    prompt_len,
    image_at,
    grid_sizes,
    image_owner,
    norm_gain,
    qkv_weight,
):
    requests = lax.axis_size(REQ)
    device_index = lax.axis_index(REQ)
    feature_width = vit_context.shape[1]
    merged_context = jnp.mean(
        vit_context.astype(jnp.float32).reshape(-1, 4, feature_width), axis=1
    ).astype(jnp.bfloat16)
    merged_residual = jnp.mean(
        vision_residual.astype(jnp.float32).reshape(-1, 4, feature_width), axis=1
    )
    own_half = gather_plane(out_weight)
    other_half = lax.ppermute(own_half, "rc", [(0, 1), (1, 0)])
    core = lax.axis_index("rc")
    own_part = jnp.einsum(
        "gk,xykn->gxyn", merged_context, own_half, preferred_element_type=jnp.float32
    )
    other_part = jnp.einsum(
        "gk,xykn->gxyn", merged_context, other_half, preferred_element_type=jnp.float32
    )
    partial_value = jnp.stack(
        [jnp.where(core == 0, own_part, other_part), jnp.where(core == 0, other_part, own_part)],
        axis=3,
    ).astype(jnp.bfloat16)
    partial_value = jnp.roll(partial_value, lax.axis_index("rx"), axis=1)
    partial_value = jnp.roll(partial_value, lax.axis_index("ry"), axis=2)
    partial_value = partial_value.reshape(own_part.shape[0], -1)
    tp_count = lax.axis_size("tp")
    block_terms = partial_value.astype(jnp.bfloat16).reshape(
        -1, tp_count, feature_width
    ).transpose(1, 0, 2)
    own_share = jnp.sum(
        lax.all_to_all(block_terms, "tp", 0, 0, tiled=True).astype(jnp.float32), axis=0
    )
    merged = (merged_residual + layer_scale[None, :] * own_share).astype(jnp.bfloat16)
    merged_count = merged.shape[0]
    counts, starts = request_plan(grid_sizes, image_owner, requests)
    request_ends = starts + counts
    capacity = (IMG_MAX + requests - 1) // requests
    request_ids = jnp.arange(requests, dtype=jnp.int32)
    group_index = jnp.arange(merged_count, dtype=jnp.int32) * requests + device_index
    destination = jnp.sum((request_ends[None, :] <= group_index[:, None]).astype(jnp.int32), axis=1)
    owned_start = jnp.sum(
        jnp.where(destination[:, None] == request_ids[None, :], starts[None, :], 0), axis=1
    )
    target = destination * capacity + (group_index - owned_start) // requests
    usable = destination < requests
    send_slots = jnp.arange(requests * capacity, dtype=jnp.int32)
    placing = ((send_slots[:, None] == target[None, :]) & usable[None, :]).astype(jnp.bfloat16)
    outgoing = jnp.dot(placing, merged, preferred_element_type=jnp.float32).astype(jnp.bfloat16)
    arrived = lax.all_to_all(
        outgoing.reshape(requests, capacity, feature_width),
        REQ,
        split_axis=0,
        concat_axis=0,
        tiled=True,
    )
    arrived = arrived.reshape(requests * capacity, feature_width)
    own_request = request_ids == device_index
    own_count = jnp.sum(jnp.where(own_request, counts, 0))
    own_start = jnp.sum(jnp.where(own_request, starts, 0))
    image_from = image_at[0]
    prompt_count = prompt_len[0]
    seq_slots = prompt.shape[1] + IMG_MAX
    slot_index = jnp.arange(seq_slots, dtype=jnp.int32)
    image_row = slot_index - image_from
    in_image = (image_row >= 0) & (image_row < own_count)
    is_live = slot_index < prompt_count + own_count
    from_prompt = is_live & jnp.logical_not(in_image)
    prompt_row = jnp.where(slot_index < image_from, slot_index, slot_index - own_count)
    prompt_ids = jnp.arange(prompt.shape[1], dtype=jnp.int32)
    prompt_pick = ((prompt_row[:, None] == prompt_ids[None, :]) & from_prompt[:, None]).astype(
        jnp.bfloat16
    )
    full_image = gather_features(arrived, tp_count)
    full_prompt = lax.all_gather(prompt[0], "tp", axis=1, tiled=True)
    full_weight = lax.all_gather(qkv_weight, REQ, axis=0, tiled=True)
    cosine_table, sine_table = rope_tables(seq_slots)
    prompt_rows = jnp.dot(prompt_pick, full_prompt, preferred_element_type=jnp.float32)
    prompt_normed = normalize(prompt_rows.astype(jnp.bfloat16), norm_gain)
    prompt_out = apply_rope(
        jnp.dot(prompt_normed, full_weight, preferred_element_type=jnp.float32),
        cosine_table,
        sine_table,
    ).astype(jnp.bfloat16)
    image_ids = jnp.arange(IMG_MAX, dtype=jnp.int32)
    image_flat = (own_start + image_ids) % requests * capacity + image_ids // requests
    image_order = (
        (image_flat[:, None] == send_slots[None, :]) & (image_ids < own_count)[:, None]
    ).astype(jnp.bfloat16)
    image_rows = jnp.dot(image_order, full_image, preferred_element_type=jnp.float32)
    image_normed = normalize(image_rows.astype(jnp.bfloat16), norm_gain)
    image_out = apply_rope(
        jnp.dot(image_normed, full_weight, preferred_element_type=jnp.float32),
        lax.dynamic_slice_in_dim(cosine_table, image_from, IMG_MAX, 0),
        lax.dynamic_slice_in_dim(sine_table, image_from, IMG_MAX, 0),
    ).astype(jnp.bfloat16)
    image_place = ((image_row[:, None] == image_ids[None, :]) & in_image[:, None]).astype(
        jnp.bfloat16
    )
    placed = jnp.dot(image_place, image_out, preferred_element_type=jnp.float32)
    return jnp.where(in_image[:, None], placed.astype(jnp.bfloat16), prompt_out)


def solution(mesh):
    in_specs = (
        P("req", "tp"),
        P("req", "tp"),
        P("tp", "req"),
        P("tp"),
        P("req", None, "tp"),
        P("req"),
        P("req"),
        P(),
        P(),
        P(),
        P("req", "tp"),
    )
    out_specs = P("req", "tp")
    rows, columns = mesh.devices.shape
    x_size = len({device.coords[0] for device in mesh.devices.flat})
    split_mesh = Mesh(
        mesh.devices.reshape(x_size, rows // (2 * x_size), 2, columns), REQ + ("tp",)
    )
    rename = lambda spec: P(*(REQ if axis == "req" else axis for axis in spec))
    return jax.shard_map(
        shards,
        mesh=split_mesh,
        in_specs=tuple(rename(spec) for spec in in_specs),
        out_specs=rename(out_specs),
        check_vma=False,
    )
```

```python
import jax
import jax.numpy as jnp
from jax import lax
from jax.sharding import Mesh, PartitionSpec as P

HEAD = 128
GROUP = 4
IMG_MAX = 128
REQ = ("rx", "ry", "rc")


def request_plan(grid_sizes, image_owner, requests):
    image_rows = grid_sizes[:, 0] * grid_sizes[:, 1]
    member = (image_owner[:, None] == jnp.arange(requests, dtype=jnp.int32)[None, :]).astype(
        jnp.int32
    )
    counts = jnp.sum(image_rows[:, None] * member, axis=0)
    starts = jnp.cumsum(counts) - counts
    return (counts, starts)


def rope_tables(count):
    half_size = HEAD // 2
    exponent = jnp.arange(half_size, dtype=jnp.float32) * (2.0 / HEAD)
    frequency = jnp.exp(-exponent * jnp.log(jnp.float32(500000.0)))
    angles = jnp.arange(count, dtype=jnp.float32)[:, None] * frequency[None, :]
    return (jnp.cos(angles), jnp.sin(angles))


def apply_rope(projected, cosine_table, sine_table):
    seq_rows = projected.shape[0]
    head_blocks = projected.reshape(seq_rows, -1, GROUP + 2, HEAD)
    turning = head_blocks[:, :, : GROUP + 1, :]
    first_half = turning[..., : HEAD // 2]
    second_half = turning[..., HEAD // 2 :]
    cosine_wide = cosine_table[:, None, None, :]
    sine_wide = sine_table[:, None, None, :]
    turned = jnp.concatenate(
        [
            first_half * cosine_wide - second_half * sine_wide,
            second_half * cosine_wide + first_half * sine_wide,
        ],
        axis=-1,
    )
    head_blocks = jnp.concatenate([turned, head_blocks[:, :, GROUP + 1 :, :]], axis=2)
    return head_blocks.reshape(seq_rows, -1)


def normalize(embedded, norm_gain):
    values = embedded.astype(jnp.float32)
    mean_square = jnp.mean(values * values, axis=-1, keepdims=True)
    return (values * lax.rsqrt(mean_square + 1e-05) * norm_gain[None, :]).astype(jnp.bfloat16)


def gather_features(rows, tp_count):
    copies = jnp.broadcast_to(rows[None], (tp_count,) + rows.shape)
    blocks = lax.all_to_all(copies, "tp", 0, 0, tiled=True)
    return blocks.transpose(1, 0, 2).reshape(rows.shape[0], -1)


def shift(value, axis, step):
    size = lax.axis_size(axis)
    return lax.ppermute(value, axis, [(k, (k + step) % size) for k in range(size)])


def ring_gather(value, axis):
    size = lax.axis_size(axis)
    return jnp.stack([value] + [shift(value, axis, -step) for step in range(1, size)], axis=0)


def gather_plane(shard):
    by_y = ring_gather(shard, "ry")
    return ring_gather(by_y, "rx")


def shards(
    vit_context,
    vision_residual,
    out_weight,
    layer_scale,
    prompt,
    prompt_len,
    image_at,
    grid_sizes,
    image_owner,
    norm_gain,
    qkv_weight,
):
    requests = lax.axis_size(REQ)
    device_index = lax.axis_index(REQ)
    feature_width = vit_context.shape[1]
    merged_context = jnp.mean(
        vit_context.astype(jnp.float32).reshape(-1, 4, feature_width), axis=1
    ).astype(jnp.bfloat16)
    merged_residual = jnp.mean(
        vision_residual.astype(jnp.float32).reshape(-1, 4, feature_width), axis=1
    )
    own_half = gather_plane(out_weight)
    other_half = lax.ppermute(own_half, "rc", [(0, 1), (1, 0)])
    core = lax.axis_index("rc")
    own_part = jnp.einsum(
        "gk,xykn->gxyn", merged_context, own_half, preferred_element_type=jnp.float32
    )
    other_part = jnp.einsum(
        "gk,xykn->gxyn", merged_context, other_half, preferred_element_type=jnp.float32
    )
    partial_value = jnp.stack(
        [jnp.where(core == 0, own_part, other_part), jnp.where(core == 0, other_part, own_part)],
        axis=3,
    ).astype(jnp.bfloat16)
    partial_value = jnp.roll(partial_value, lax.axis_index("rx"), axis=1)
    partial_value = jnp.roll(partial_value, lax.axis_index("ry"), axis=2)
    partial_value = partial_value.reshape(own_part.shape[0], -1)
    tp_count = lax.axis_size("tp")
    block_terms = partial_value.astype(jnp.bfloat16).reshape(
        -1, tp_count, feature_width
    ).transpose(1, 0, 2)
    own_share = jnp.sum(
        lax.all_to_all(block_terms, "tp", 0, 0, tiled=True).astype(jnp.float32), axis=0
    )
    merged = (merged_residual + layer_scale[None, :] * own_share).astype(jnp.bfloat16)
    merged_count = merged.shape[0]
    counts, starts = request_plan(grid_sizes, image_owner, requests)
    request_ends = starts + counts
    capacity = (IMG_MAX + requests - 1) // requests
    request_ids = jnp.arange(requests, dtype=jnp.int32)
    group_index = jnp.arange(merged_count, dtype=jnp.int32) * requests + device_index
    destination = jnp.sum((request_ends[None, :] <= group_index[:, None]).astype(jnp.int32), axis=1)
    owned_start = jnp.sum(
        jnp.where(destination[:, None] == request_ids[None, :], starts[None, :], 0), axis=1
    )
    target = destination * capacity + (group_index - owned_start) // requests
    usable = destination < requests
    send_slots = jnp.arange(requests * capacity, dtype=jnp.int32)
    placing = ((send_slots[:, None] == target[None, :]) & usable[None, :]).astype(jnp.bfloat16)
    outgoing = jnp.dot(placing, merged, preferred_element_type=jnp.float32).astype(jnp.bfloat16)
    arrived = lax.all_to_all(
        outgoing.reshape(requests, capacity, feature_width),
        REQ,
        split_axis=0,
        concat_axis=0,
        tiled=True,
    )
    arrived = arrived.reshape(requests * capacity, feature_width)
    own_request = request_ids == device_index
    own_count = jnp.sum(jnp.where(own_request, counts, 0))
    own_start = jnp.sum(jnp.where(own_request, starts, 0))
    image_from = image_at[0]
    prompt_count = prompt_len[0]
    seq_slots = prompt.shape[1] + IMG_MAX
    slot_index = jnp.arange(seq_slots, dtype=jnp.int32)
    image_row = slot_index - image_from
    in_image = (image_row >= 0) & (image_row < own_count)
    is_live = slot_index < prompt_count + own_count
    from_prompt = is_live & jnp.logical_not(in_image)
    prompt_row = jnp.where(slot_index < image_from, slot_index, slot_index - own_count)
    prompt_ids = jnp.arange(prompt.shape[1], dtype=jnp.int32)
    prompt_pick = ((prompt_row[:, None] == prompt_ids[None, :]) & from_prompt[:, None]).astype(
        jnp.bfloat16
    )
    full_image = gather_features(arrived, tp_count)
    full_prompt = lax.all_gather(prompt[0], "tp", axis=1, tiled=True)
    full_weight = lax.all_gather(qkv_weight, REQ, axis=0, tiled=True)
    cosine_table, sine_table = rope_tables(seq_slots)
    prompt_rows = jnp.dot(prompt_pick, full_prompt, preferred_element_type=jnp.float32)
    prompt_normed = normalize(prompt_rows.astype(jnp.bfloat16), norm_gain)
    prompt_out = apply_rope(
        jnp.dot(prompt_normed, full_weight, preferred_element_type=jnp.float32),
        cosine_table,
        sine_table,
    ).astype(jnp.bfloat16)
    image_ids = jnp.arange(IMG_MAX, dtype=jnp.int32)
    image_flat = (own_start + image_ids) % requests * capacity + image_ids // requests
    image_order = (
        (image_flat[:, None] == send_slots[None, :]) & (image_ids < own_count)[:, None]
    ).astype(jnp.bfloat16)
    full_image, prompt_out = lax.optimization_barrier((full_image, prompt_out))
    image_rows = jnp.dot(image_order, full_image, preferred_element_type=jnp.float32)
    image_normed = normalize(image_rows.astype(jnp.bfloat16), norm_gain)
    image_out = apply_rope(
        jnp.dot(image_normed, full_weight, preferred_element_type=jnp.float32),
        lax.dynamic_slice_in_dim(cosine_table, image_from, IMG_MAX, 0),
        lax.dynamic_slice_in_dim(sine_table, image_from, IMG_MAX, 0),
    ).astype(jnp.bfloat16)
    image_place = ((image_row[:, None] == image_ids[None, :]) & in_image[:, None]).astype(
        jnp.bfloat16
    )
    placed = jnp.dot(image_place, image_out, preferred_element_type=jnp.float32)
    return jnp.where(in_image[:, None], placed.astype(jnp.bfloat16), prompt_out)


def solution(mesh):
    in_specs = (
        P("req", "tp"),
        P("req", "tp"),
        P("tp", "req"),
        P("tp"),
        P("req", None, "tp"),
        P("req"),
        P("req"),
        P(),
        P(),
        P(),
        P("req", "tp"),
    )
    out_specs = P("req", "tp")
    rows, columns = mesh.devices.shape
    x_size = len({device.coords[0] for device in mesh.devices.flat})
    split_mesh = Mesh(
        mesh.devices.reshape(x_size, rows // (2 * x_size), 2, columns), REQ + ("tp",)
    )
    rename = lambda spec: P(*(REQ if axis == "req" else axis for axis in spec))
    return jax.shard_map(
        shards,
        mesh=split_mesh,
        in_specs=tuple(rename(spec) for spec in in_specs),
        out_specs=rename(out_specs),
        check_vma=False,
    )
```

```python
import jax
import jax.numpy as jnp
from jax import lax
from jax.sharding import Mesh, PartitionSpec as P

HEAD = 128
GROUP = 4
IMG_MAX = 128
REQ = ("rx", "ry", "rc")


def request_plan(grid_sizes, image_owner, requests):
    image_rows = grid_sizes[:, 0] * grid_sizes[:, 1]
    member = (image_owner[:, None] == jnp.arange(requests, dtype=jnp.int32)[None, :]).astype(
        jnp.int32
    )
    counts = jnp.sum(image_rows[:, None] * member, axis=0)
    starts = jnp.cumsum(counts) - counts
    return (counts, starts)


def rope_tables(count):
    half_size = HEAD // 2
    exponent = jnp.arange(half_size, dtype=jnp.float32) * (2.0 / HEAD)
    frequency = jnp.exp(-exponent * jnp.log(jnp.float32(500000.0)))
    angles = jnp.arange(count, dtype=jnp.float32)[:, None] * frequency[None, :]
    return (jnp.cos(angles), jnp.sin(angles))


def apply_rope(projected, cosine_table, sine_table):
    seq_rows = projected.shape[0]
    head_blocks = projected.reshape(seq_rows, -1, GROUP + 2, HEAD)
    turning = head_blocks[:, :, : GROUP + 1, :]
    first_half = turning[..., : HEAD // 2]
    second_half = turning[..., HEAD // 2 :]
    cosine_wide = cosine_table[:, None, None, :]
    sine_wide = sine_table[:, None, None, :]
    turned = jnp.concatenate(
        [
            first_half * cosine_wide - second_half * sine_wide,
            second_half * cosine_wide + first_half * sine_wide,
        ],
        axis=-1,
    )
    head_blocks = jnp.concatenate([turned, head_blocks[:, :, GROUP + 1 :, :]], axis=2)
    return head_blocks.reshape(seq_rows, -1)


def normalize(embedded, norm_gain):
    values = embedded.astype(jnp.float32)
    mean_square = jnp.mean(values * values, axis=-1, keepdims=True)
    return (values * lax.rsqrt(mean_square + 1e-05) * norm_gain[None, :]).astype(jnp.bfloat16)


def gather_features(rows, tp_count):
    copies = jnp.broadcast_to(rows[None], (tp_count,) + rows.shape)
    blocks = lax.all_to_all(copies, "tp", 0, 0, tiled=True)
    return blocks.transpose(1, 0, 2).reshape(rows.shape[0], -1)


def shift(value, axis, step):
    size = lax.axis_size(axis)
    return lax.ppermute(value, axis, [(k, (k + step) % size) for k in range(size)])


def ring_gather(value, axis):
    size = lax.axis_size(axis)
    return jnp.stack([value] + [shift(value, axis, -step) for step in range(1, size)], axis=0)


def eight_gather(value, axis):
    from_next = shift(value, axis, -1)
    from_last = shift(value, axis, 1)
    three = jnp.stack([from_last, value, from_next], axis=0)
    far_next = shift(three, axis, -3)
    far_last = shift(three, axis, 3)
    return jnp.stack(
        [value, from_next, far_next[0], far_next[1], far_next[2], far_last[1], far_last[2], from_last],
        axis=0,
    )


def gather_plane(shard):
    by_y = eight_gather(shard, "ry") if lax.axis_size("ry") == 8 else ring_gather(shard, "ry")
    return ring_gather(by_y, "rx")


def shards(
    vit_context,
    vision_residual,
    out_weight,
    layer_scale,
    prompt,
    prompt_len,
    image_at,
    grid_sizes,
    image_owner,
    norm_gain,
    qkv_weight,
):
    requests = lax.axis_size(REQ)
    device_index = lax.axis_index(REQ)
    feature_width = vit_context.shape[1]
    merged_context = jnp.mean(
        vit_context.astype(jnp.float32).reshape(-1, 4, feature_width), axis=1
    ).astype(jnp.bfloat16)
    merged_residual = jnp.mean(
        vision_residual.astype(jnp.float32).reshape(-1, 4, feature_width), axis=1
    )
    own_half = gather_plane(out_weight)
    other_half = lax.ppermute(own_half, "rc", [(0, 1), (1, 0)])
    core = lax.axis_index("rc")
    own_part = jnp.einsum(
        "gk,xykn->gxyn", merged_context, own_half, preferred_element_type=jnp.float32
    )
    other_part = jnp.einsum(
        "gk,xykn->gxyn", merged_context, other_half, preferred_element_type=jnp.float32
    )
    partial_value = jnp.stack(
        [jnp.where(core == 0, own_part, other_part), jnp.where(core == 0, other_part, own_part)],
        axis=3,
    ).astype(jnp.bfloat16)
    partial_value = jnp.roll(partial_value, lax.axis_index("rx"), axis=1)
    partial_value = jnp.roll(partial_value, lax.axis_index("ry"), axis=2)
    partial_value = partial_value.reshape(own_part.shape[0], -1)
    tp_count = lax.axis_size("tp")
    block_terms = partial_value.astype(jnp.bfloat16).reshape(
        -1, tp_count, feature_width
    ).transpose(1, 0, 2)
    own_share = jnp.sum(
        lax.all_to_all(block_terms, "tp", 0, 0, tiled=True).astype(jnp.float32), axis=0
    )
    merged = (merged_residual + layer_scale[None, :] * own_share).astype(jnp.bfloat16)
    merged_count = merged.shape[0]
    counts, starts = request_plan(grid_sizes, image_owner, requests)
    request_ends = starts + counts
    capacity = (IMG_MAX + requests - 1) // requests
    request_ids = jnp.arange(requests, dtype=jnp.int32)
    group_index = jnp.arange(merged_count, dtype=jnp.int32) * requests + device_index
    destination = jnp.sum((request_ends[None, :] <= group_index[:, None]).astype(jnp.int32), axis=1)
    owned_start = jnp.sum(
        jnp.where(destination[:, None] == request_ids[None, :], starts[None, :], 0), axis=1
    )
    target = destination * capacity + (group_index - owned_start) // requests
    usable = destination < requests
    send_slots = jnp.arange(requests * capacity, dtype=jnp.int32)
    placing = ((send_slots[:, None] == target[None, :]) & usable[None, :]).astype(jnp.bfloat16)
    outgoing = jnp.dot(placing, merged, preferred_element_type=jnp.float32).astype(jnp.bfloat16)
    arrived = lax.all_to_all(
        outgoing.reshape(requests, capacity, feature_width),
        REQ,
        split_axis=0,
        concat_axis=0,
        tiled=True,
    )
    arrived = arrived.reshape(requests * capacity, feature_width)
    own_request = request_ids == device_index
    own_count = jnp.sum(jnp.where(own_request, counts, 0))
    own_start = jnp.sum(jnp.where(own_request, starts, 0))
    image_from = image_at[0]
    prompt_count = prompt_len[0]
    seq_slots = prompt.shape[1] + IMG_MAX
    slot_index = jnp.arange(seq_slots, dtype=jnp.int32)
    image_row = slot_index - image_from
    in_image = (image_row >= 0) & (image_row < own_count)
    is_live = slot_index < prompt_count + own_count
    from_prompt = is_live & jnp.logical_not(in_image)
    prompt_row = jnp.where(slot_index < image_from, slot_index, slot_index - own_count)
    prompt_ids = jnp.arange(prompt.shape[1], dtype=jnp.int32)
    prompt_pick = ((prompt_row[:, None] == prompt_ids[None, :]) & from_prompt[:, None]).astype(
        jnp.bfloat16
    )
    full_image = gather_features(arrived, tp_count)
    full_prompt = lax.all_gather(prompt[0], "tp", axis=1, tiled=True)
    full_weight = lax.all_gather(qkv_weight, REQ, axis=0, tiled=True)
    cosine_table, sine_table = rope_tables(seq_slots)
    prompt_rows = jnp.dot(prompt_pick, full_prompt, preferred_element_type=jnp.float32)
    prompt_normed = normalize(prompt_rows.astype(jnp.bfloat16), norm_gain)
    prompt_out = apply_rope(
        jnp.dot(prompt_normed, full_weight, preferred_element_type=jnp.float32),
        cosine_table,
        sine_table,
    ).astype(jnp.bfloat16)
    image_ids = jnp.arange(IMG_MAX, dtype=jnp.int32)
    image_flat = (own_start + image_ids) % requests * capacity + image_ids // requests
    image_order = (
        (image_flat[:, None] == send_slots[None, :]) & (image_ids < own_count)[:, None]
    ).astype(jnp.bfloat16)
    full_image, prompt_out = lax.optimization_barrier((full_image, prompt_out))
    image_rows = jnp.dot(image_order, full_image, preferred_element_type=jnp.float32)
    image_normed = normalize(image_rows.astype(jnp.bfloat16), norm_gain)
    image_out = apply_rope(
        jnp.dot(image_normed, full_weight, preferred_element_type=jnp.float32),
        lax.dynamic_slice_in_dim(cosine_table, image_from, IMG_MAX, 0),
        lax.dynamic_slice_in_dim(sine_table, image_from, IMG_MAX, 0),
    ).astype(jnp.bfloat16)
    image_place = ((image_row[:, None] == image_ids[None, :]) & in_image[:, None]).astype(
        jnp.bfloat16
    )
    placed = jnp.dot(image_place, image_out, preferred_element_type=jnp.float32)
    return jnp.where(in_image[:, None], placed.astype(jnp.bfloat16), prompt_out)


def solution(mesh):
    in_specs = (
        P("req", "tp"),
        P("req", "tp"),
        P("tp", "req"),
        P("tp"),
        P("req", None, "tp"),
        P("req"),
        P("req"),
        P(),
        P(),
        P(),
        P("req", "tp"),
    )
    out_specs = P("req", "tp")
    rows, columns = mesh.devices.shape
    x_size = len({device.coords[0] for device in mesh.devices.flat})
    split_mesh = Mesh(
        mesh.devices.reshape(x_size, rows // (2 * x_size), 2, columns), REQ + ("tp",)
    )
    rename = lambda spec: P(*(REQ if axis == "req" else axis for axis in spec))
    return jax.shard_map(
        shards,
        mesh=split_mesh,
        in_specs=tuple(rename(spec) for spec in in_specs),
        out_specs=rename(out_specs),
        check_vma=False,
    )
```

```python
import jax
import jax.numpy as jnp
from jax import lax
from jax.sharding import Mesh, PartitionSpec as P

HEAD = 128
GROUP = 4
IMG_MAX = 128
REQ = ("rx", "ry", "rc")


def request_plan(grid_sizes, image_owner, requests):
    image_rows = grid_sizes[:, 0] * grid_sizes[:, 1]
    member = (image_owner[:, None] == jnp.arange(requests, dtype=jnp.int32)[None, :]).astype(
        jnp.int32
    )
    counts = jnp.sum(image_rows[:, None] * member, axis=0)
    starts = jnp.cumsum(counts) - counts
    return (counts, starts)


def rope_tables(count):
    half_size = HEAD // 2
    exponent = jnp.arange(half_size, dtype=jnp.float32) * (2.0 / HEAD)
    frequency = jnp.exp(-exponent * jnp.log(jnp.float32(500000.0)))
    angles = jnp.arange(count, dtype=jnp.float32)[:, None] * frequency[None, :]
    return (jnp.cos(angles), jnp.sin(angles))


def apply_rope(projected, cosine_table, sine_table):
    seq_rows = projected.shape[0]
    head_blocks = projected.reshape(seq_rows, -1, GROUP + 2, HEAD)
    turning = head_blocks[:, :, : GROUP + 1, :]
    first_half = turning[..., : HEAD // 2]
    second_half = turning[..., HEAD // 2 :]
    cosine_wide = cosine_table[:, None, None, :]
    sine_wide = sine_table[:, None, None, :]
    turned = jnp.concatenate(
        [
            first_half * cosine_wide - second_half * sine_wide,
            second_half * cosine_wide + first_half * sine_wide,
        ],
        axis=-1,
    )
    head_blocks = jnp.concatenate([turned, head_blocks[:, :, GROUP + 1 :, :]], axis=2)
    return head_blocks.reshape(seq_rows, -1)


def normalize(embedded, norm_gain):
    values = embedded.astype(jnp.float32)
    mean_square = jnp.mean(values * values, axis=-1, keepdims=True)
    return (values * lax.rsqrt(mean_square + 1e-05) * norm_gain[None, :]).astype(jnp.bfloat16)


def gather_features(rows, tp_count):
    copies = jnp.broadcast_to(rows[None], (tp_count,) + rows.shape)
    blocks = lax.all_to_all(copies, "tp", 0, 0, tiled=True)
    return blocks.transpose(1, 0, 2).reshape(rows.shape[0], -1)


def shift(value, axis, step):
    size = lax.axis_size(axis)
    return lax.ppermute(value, axis, [(k, (k + step) % size) for k in range(size)])


def ring_gather(value, axis):
    size = lax.axis_size(axis)
    return jnp.stack([value] + [shift(value, axis, -step) for step in range(1, size)], axis=0)


def eight_gather(value, axis):
    from_next = shift(value, axis, -1)
    from_last = shift(value, axis, 1)
    three = jnp.stack([from_last, value, from_next], axis=0)
    far_next = shift(three, axis, -3)
    far_last = shift(three, axis, 3)
    return jnp.stack(
        [value, from_next, far_next[0], far_next[1], far_next[2], far_last[1], far_last[2], from_last],
        axis=0,
    )


def gather_plane(shard):
    by_y = eight_gather(shard, "ry") if lax.axis_size("ry") == 8 else ring_gather(shard, "ry")
    return ring_gather(by_y, "rx")


def shards(
    vit_context,
    vision_residual,
    out_weight,
    layer_scale,
    prompt,
    prompt_len,
    image_at,
    grid_sizes,
    image_owner,
    norm_gain,
    qkv_weight,
):
    requests = lax.axis_size(REQ)
    device_index = lax.axis_index(REQ)
    feature_width = vit_context.shape[1]
    merged_context = jnp.mean(
        vit_context.astype(jnp.float32).reshape(-1, 4, feature_width), axis=1
    ).astype(jnp.bfloat16)
    merged_residual = jnp.mean(
        vision_residual.astype(jnp.float32).reshape(-1, 4, feature_width), axis=1
    )
    own_half = gather_plane(out_weight)
    other_half = lax.ppermute(own_half, "rc", [(0, 1), (1, 0)])
    core = lax.axis_index("rc")
    own_part = jnp.einsum(
        "gk,xykn->gxyn", merged_context, own_half, preferred_element_type=jnp.float32
    )
    other_part = jnp.einsum(
        "gk,xykn->gxyn", merged_context, other_half, preferred_element_type=jnp.float32
    )
    partial_value = jnp.stack(
        [jnp.where(core == 0, own_part, other_part), jnp.where(core == 0, other_part, own_part)],
        axis=3,
    ).astype(jnp.bfloat16)
    partial_value = jnp.roll(partial_value, lax.axis_index("rx"), axis=1)
    partial_value = jnp.roll(partial_value, lax.axis_index("ry"), axis=2)
    partial_value = partial_value.reshape(own_part.shape[0], -1)
    tp_count = lax.axis_size("tp")
    block_terms = partial_value.astype(jnp.bfloat16).reshape(
        -1, tp_count, feature_width
    ).transpose(1, 0, 2)
    own_share = jnp.sum(
        lax.all_to_all(block_terms, "tp", 0, 0, tiled=True).astype(jnp.float32), axis=0
    )
    merged = (merged_residual + layer_scale[None, :] * own_share).astype(jnp.bfloat16)
    merged_count = merged.shape[0]
    counts, starts = request_plan(grid_sizes, image_owner, requests)
    request_ends = starts + counts
    capacity = (IMG_MAX + requests - 1) // requests
    request_ids = jnp.arange(requests, dtype=jnp.int32)
    group_index = jnp.arange(merged_count, dtype=jnp.int32) * requests + device_index
    destination = jnp.sum((request_ends[None, :] <= group_index[:, None]).astype(jnp.int32), axis=1)
    owned_start = jnp.sum(
        jnp.where(destination[:, None] == request_ids[None, :], starts[None, :], 0), axis=1
    )
    target = destination * capacity + (group_index - owned_start) // requests
    usable = destination < requests
    send_slots = jnp.arange(requests * capacity, dtype=jnp.int32)
    placing = ((send_slots[:, None] == target[None, :]) & usable[None, :]).astype(jnp.bfloat16)
    outgoing = jnp.dot(placing, merged, preferred_element_type=jnp.float32).astype(jnp.bfloat16)
    arrived = lax.all_to_all(
        outgoing.reshape(requests, capacity, feature_width),
        REQ,
        split_axis=0,
        concat_axis=0,
        tiled=True,
    )
    arrived = arrived.reshape(requests * capacity, feature_width)
    own_request = request_ids == device_index
    own_count = jnp.sum(jnp.where(own_request, counts, 0))
    own_start = jnp.sum(jnp.where(own_request, starts, 0))
    image_from = image_at[0]
    prompt_count = prompt_len[0]
    seq_slots = prompt.shape[1] + IMG_MAX
    slot_index = jnp.arange(seq_slots, dtype=jnp.int32)
    image_row = slot_index - image_from
    in_image = (image_row >= 0) & (image_row < own_count)
    is_live = slot_index < prompt_count + own_count
    from_prompt = is_live & jnp.logical_not(in_image)
    prompt_row = jnp.where(slot_index < image_from, slot_index, slot_index - own_count)
    prompt_ids = jnp.arange(prompt.shape[1], dtype=jnp.int32)
    prompt_pick = ((prompt_row[:, None] == prompt_ids[None, :]) & from_prompt[:, None]).astype(
        jnp.bfloat16
    )
    full_prompt = lax.all_gather(prompt[0], "tp", axis=1, tiled=True)
    full_weight = lax.all_gather(qkv_weight, REQ, axis=0, tiled=True)
    cosine_table, sine_table = rope_tables(seq_slots)
    prompt_rows = jnp.dot(prompt_pick, full_prompt, preferred_element_type=jnp.float32)
    prompt_normed = normalize(prompt_rows.astype(jnp.bfloat16), norm_gain)
    prompt_out = apply_rope(
        jnp.dot(prompt_normed, full_weight, preferred_element_type=jnp.float32),
        cosine_table,
        sine_table,
    ).astype(jnp.bfloat16)
    image_ids = jnp.arange(IMG_MAX, dtype=jnp.int32)
    image_flat = (own_start + image_ids) % requests * capacity + image_ids // requests
    image_order = (
        (image_flat[:, None] == send_slots[None, :]) & (image_ids < own_count)[:, None]
    ).astype(jnp.bfloat16)
    ordered = jnp.dot(image_order, arrived, preferred_element_type=jnp.float32)
    image_rows = gather_features(ordered.astype(jnp.bfloat16), tp_count)
    image_rows, prompt_out = lax.optimization_barrier((image_rows, prompt_out))
    image_normed = normalize(image_rows, norm_gain)
    image_out = apply_rope(
        jnp.dot(image_normed, full_weight, preferred_element_type=jnp.float32),
        lax.dynamic_slice_in_dim(cosine_table, image_from, IMG_MAX, 0),
        lax.dynamic_slice_in_dim(sine_table, image_from, IMG_MAX, 0),
    ).astype(jnp.bfloat16)
    image_place = ((image_row[:, None] == image_ids[None, :]) & in_image[:, None]).astype(
        jnp.bfloat16
    )
    placed = jnp.dot(image_place, image_out, preferred_element_type=jnp.float32)
    return jnp.where(in_image[:, None], placed.astype(jnp.bfloat16), prompt_out)


def solution(mesh):
    in_specs = (
        P("req", "tp"),
        P("req", "tp"),
        P("tp", "req"),
        P("tp"),
        P("req", None, "tp"),
        P("req"),
        P("req"),
        P(),
        P(),
        P(),
        P("req", "tp"),
    )
    out_specs = P("req", "tp")
    rows, columns = mesh.devices.shape
    x_size = len({device.coords[0] for device in mesh.devices.flat})
    split_mesh = Mesh(
        mesh.devices.reshape(x_size, rows // (2 * x_size), 2, columns), REQ + ("tp",)
    )
    rename = lambda spec: P(*(REQ if axis == "req" else axis for axis in spec))
    return jax.shard_map(
        shards,
        mesh=split_mesh,
        in_specs=tuple(rename(spec) for spec in in_specs),
        out_specs=rename(out_specs),
        check_vma=False,
    )
```

```python
import jax
import jax.numpy as jnp
from jax import lax
from jax.sharding import Mesh, PartitionSpec as P

HEAD = 128
GROUP = 4
IMG_MAX = 128
REQ = ("rx", "ry", "rc")


def request_plan(grid_sizes, image_owner, requests):
    image_rows = grid_sizes[:, 0] * grid_sizes[:, 1]
    member = (image_owner[:, None] == jnp.arange(requests, dtype=jnp.int32)[None, :]).astype(
        jnp.int32
    )
    counts = jnp.sum(image_rows[:, None] * member, axis=0)
    starts = jnp.cumsum(counts) - counts
    return (counts, starts)


def rope_tables(count):
    half_size = HEAD // 2
    exponent = jnp.arange(half_size, dtype=jnp.float32) * (2.0 / HEAD)
    frequency = jnp.exp(-exponent * jnp.log(jnp.float32(500000.0)))
    angles = jnp.arange(count, dtype=jnp.float32)[:, None] * frequency[None, :]
    return (jnp.cos(angles), jnp.sin(angles))


def apply_rope(projected, cosine_table, sine_table):
    seq_rows = projected.shape[0]
    head_blocks = projected.reshape(seq_rows, -1, GROUP + 2, HEAD)
    turning = head_blocks[:, :, : GROUP + 1, :]
    first_half = turning[..., : HEAD // 2]
    second_half = turning[..., HEAD // 2 :]
    cosine_wide = cosine_table[:, None, None, :]
    sine_wide = sine_table[:, None, None, :]
    turned = jnp.concatenate(
        [
            first_half * cosine_wide - second_half * sine_wide,
            second_half * cosine_wide + first_half * sine_wide,
        ],
        axis=-1,
    )
    head_blocks = jnp.concatenate([turned, head_blocks[:, :, GROUP + 1 :, :]], axis=2)
    return head_blocks.reshape(seq_rows, -1)


def normalize(embedded, norm_gain):
    values = embedded.astype(jnp.float32)
    mean_square = jnp.mean(values * values, axis=-1, keepdims=True)
    return (values * lax.rsqrt(mean_square + 1e-05) * norm_gain[None, :]).astype(jnp.bfloat16)


def gather_features(rows, tp_count):
    copies = jnp.broadcast_to(rows[None], (tp_count,) + rows.shape)
    blocks = lax.all_to_all(copies, "tp", 0, 0, tiled=True)
    return blocks.transpose(1, 0, 2).reshape(rows.shape[0], -1)


def shift(value, axis, step):
    size = lax.axis_size(axis)
    return lax.ppermute(value, axis, [(k, (k + step) % size) for k in range(size)])


def ring_gather(value, axis):
    size = lax.axis_size(axis)
    return jnp.stack([value] + [shift(value, axis, -step) for step in range(1, size)], axis=0)


def eight_gather(value, axis):
    from_next = shift(value, axis, -1)
    from_last = shift(value, axis, 1)
    three = jnp.stack([from_last, value, from_next], axis=0)
    far_next = shift(three, axis, -3)
    far_last = shift(three, axis, 3)
    return jnp.stack(
        [value, from_next, far_next[0], far_next[1], far_next[2], far_last[1], far_last[2], from_last],
        axis=0,
    )


def gather_plane(shard):
    by_y = eight_gather(shard, "ry") if lax.axis_size("ry") == 8 else ring_gather(shard, "ry")
    return ring_gather(by_y, "rx")


def block_sum(part, tp_count):
    terms = part.astype(jnp.bfloat16)
    terms = jnp.roll(terms, lax.axis_index("rx"), axis=1)
    terms = jnp.roll(terms, lax.axis_index("ry"), axis=2)
    terms = terms.reshape(terms.shape[0], tp_count, -1).transpose(1, 0, 2)
    arrived = lax.all_to_all(terms, "tp", 0, 0, tiled=True)
    return jnp.sum(arrived.astype(jnp.float32), axis=0)


def shards(
    vit_context,
    vision_residual,
    out_weight,
    layer_scale,
    prompt,
    prompt_len,
    image_at,
    grid_sizes,
    image_owner,
    norm_gain,
    qkv_weight,
):
    requests = lax.axis_size(REQ)
    device_index = lax.axis_index(REQ)
    feature_width = vit_context.shape[1]
    merged_context = jnp.mean(
        vit_context.astype(jnp.float32).reshape(-1, 4, feature_width), axis=1
    ).astype(jnp.bfloat16)
    merged_residual = jnp.mean(
        vision_residual.astype(jnp.float32).reshape(-1, 4, feature_width), axis=1
    )
    own_half = gather_plane(out_weight)
    other_half = lax.ppermute(own_half, "rc", [(0, 1), (1, 0)])
    core = lax.axis_index("rc")
    own_part = jnp.einsum(
        "gk,xykn->gxyn", merged_context, own_half, preferred_element_type=jnp.float32
    )
    other_part = jnp.einsum(
        "gk,xykn->gxyn", merged_context, other_half, preferred_element_type=jnp.float32
    )
    tp_count = lax.axis_size("tp")
    own_sum = block_sum(own_part, tp_count).reshape(own_part.shape[0], -1, 1, own_part.shape[-1])
    other_sum = block_sum(other_part, tp_count).reshape(own_sum.shape)
    own_share = jnp.concatenate(
        [jnp.where(core == 0, own_sum, other_sum), jnp.where(core == 0, other_sum, own_sum)],
        axis=2,
    ).reshape(own_part.shape[0], feature_width)
    merged = (merged_residual + layer_scale[None, :] * own_share).astype(jnp.bfloat16)
    merged_count = merged.shape[0]
    counts, starts = request_plan(grid_sizes, image_owner, requests)
    request_ends = starts + counts
    capacity = (IMG_MAX + requests - 1) // requests
    request_ids = jnp.arange(requests, dtype=jnp.int32)
    group_index = jnp.arange(merged_count, dtype=jnp.int32) * requests + device_index
    destination = jnp.sum((request_ends[None, :] <= group_index[:, None]).astype(jnp.int32), axis=1)
    owned_start = jnp.sum(
        jnp.where(destination[:, None] == request_ids[None, :], starts[None, :], 0), axis=1
    )
    target = destination * capacity + (group_index - owned_start) // requests
    usable = destination < requests
    send_slots = jnp.arange(requests * capacity, dtype=jnp.int32)
    placing = ((send_slots[:, None] == target[None, :]) & usable[None, :]).astype(jnp.bfloat16)
    outgoing = jnp.dot(placing, merged, preferred_element_type=jnp.float32).astype(jnp.bfloat16)
    arrived = lax.all_to_all(
        outgoing.reshape(requests, capacity, feature_width),
        REQ,
        split_axis=0,
        concat_axis=0,
        tiled=True,
    )
    arrived = arrived.reshape(requests * capacity, feature_width)
    own_request = request_ids == device_index
    own_count = jnp.sum(jnp.where(own_request, counts, 0))
    own_start = jnp.sum(jnp.where(own_request, starts, 0))
    image_from = image_at[0]
    prompt_count = prompt_len[0]
    seq_slots = prompt.shape[1] + IMG_MAX
    slot_index = jnp.arange(seq_slots, dtype=jnp.int32)
    image_row = slot_index - image_from
    in_image = (image_row >= 0) & (image_row < own_count)
    is_live = slot_index < prompt_count + own_count
    from_prompt = is_live & jnp.logical_not(in_image)
    prompt_row = jnp.where(slot_index < image_from, slot_index, slot_index - own_count)
    prompt_ids = jnp.arange(prompt.shape[1], dtype=jnp.int32)
    prompt_pick = ((prompt_row[:, None] == prompt_ids[None, :]) & from_prompt[:, None]).astype(
        jnp.bfloat16
    )
    full_image = gather_features(arrived, tp_count)
    full_prompt = lax.all_gather(prompt[0], "tp", axis=1, tiled=True)
    full_weight = lax.all_gather(qkv_weight, REQ, axis=0, tiled=True)
    cosine_table, sine_table = rope_tables(seq_slots)
    prompt_rows = jnp.dot(prompt_pick, full_prompt, preferred_element_type=jnp.float32)
    prompt_normed = normalize(prompt_rows.astype(jnp.bfloat16), norm_gain)
    prompt_out = apply_rope(
        jnp.dot(prompt_normed, full_weight, preferred_element_type=jnp.float32),
        cosine_table,
        sine_table,
    ).astype(jnp.bfloat16)
    image_ids = jnp.arange(IMG_MAX, dtype=jnp.int32)
    image_flat = (own_start + image_ids) % requests * capacity + image_ids // requests
    image_order = (
        (image_flat[:, None] == send_slots[None, :]) & (image_ids < own_count)[:, None]
    ).astype(jnp.bfloat16)
    full_image, prompt_out = lax.optimization_barrier((full_image, prompt_out))
    image_rows = jnp.dot(image_order, full_image, preferred_element_type=jnp.float32)
    image_normed = normalize(image_rows.astype(jnp.bfloat16), norm_gain)
    image_out = apply_rope(
        jnp.dot(image_normed, full_weight, preferred_element_type=jnp.float32),
        lax.dynamic_slice_in_dim(cosine_table, image_from, IMG_MAX, 0),
        lax.dynamic_slice_in_dim(sine_table, image_from, IMG_MAX, 0),
    ).astype(jnp.bfloat16)
    image_place = ((image_row[:, None] == image_ids[None, :]) & in_image[:, None]).astype(
        jnp.bfloat16
    )
    placed = jnp.dot(image_place, image_out, preferred_element_type=jnp.float32)
    return jnp.where(in_image[:, None], placed.astype(jnp.bfloat16), prompt_out)


def solution(mesh):
    in_specs = (
        P("req", "tp"),
        P("req", "tp"),
        P("tp", "req"),
        P("tp"),
        P("req", None, "tp"),
        P("req"),
        P("req"),
        P(),
        P(),
        P(),
        P("req", "tp"),
    )
    out_specs = P("req", "tp")
    rows, columns = mesh.devices.shape
    x_size = len({device.coords[0] for device in mesh.devices.flat})
    split_mesh = Mesh(
        mesh.devices.reshape(x_size, rows // (2 * x_size), 2, columns), REQ + ("tp",)
    )
    rename = lambda spec: P(*(REQ if axis == "req" else axis for axis in spec))
    return jax.shard_map(
        shards,
        mesh=split_mesh,
        in_specs=tuple(rename(spec) for spec in in_specs),
        out_specs=rename(out_specs),
        check_vma=False,
    )
```

```python
import jax
import jax.numpy as jnp
from jax import lax
from jax.sharding import Mesh, PartitionSpec as P

HEAD = 128
GROUP = 4
IMG_MAX = 128
REQ = ("rx", "ry", "rc")


def request_plan(grid_sizes, image_owner, requests):
    image_rows = grid_sizes[:, 0] * grid_sizes[:, 1]
    member = (image_owner[:, None] == jnp.arange(requests, dtype=jnp.int32)[None, :]).astype(
        jnp.int32
    )
    counts = jnp.sum(image_rows[:, None] * member, axis=0)
    starts = jnp.cumsum(counts) - counts
    return (counts, starts)


def rope_tables(count):
    half_size = HEAD // 2
    exponent = jnp.arange(half_size, dtype=jnp.float32) * (2.0 / HEAD)
    frequency = jnp.exp(-exponent * jnp.log(jnp.float32(500000.0)))
    angles = jnp.arange(count, dtype=jnp.float32)[:, None] * frequency[None, :]
    return (jnp.cos(angles), jnp.sin(angles))


def apply_rope(projected, cosine_table, sine_table):
    seq_rows = projected.shape[0]
    head_blocks = projected.reshape(seq_rows, -1, GROUP + 2, HEAD)
    turning = head_blocks[:, :, : GROUP + 1, :]
    first_half = turning[..., : HEAD // 2]
    second_half = turning[..., HEAD // 2 :]
    cosine_wide = cosine_table[:, None, None, :]
    sine_wide = sine_table[:, None, None, :]
    turned = jnp.concatenate(
        [
            first_half * cosine_wide - second_half * sine_wide,
            second_half * cosine_wide + first_half * sine_wide,
        ],
        axis=-1,
    )
    head_blocks = jnp.concatenate([turned, head_blocks[:, :, GROUP + 1 :, :]], axis=2)
    return head_blocks.reshape(seq_rows, -1)


def normalize(embedded, norm_gain):
    values = embedded.astype(jnp.float32)
    mean_square = jnp.mean(values * values, axis=-1, keepdims=True)
    return (values * lax.rsqrt(mean_square + 1e-05) * norm_gain[None, :]).astype(jnp.bfloat16)


def gather_features(rows, tp_count):
    copies = jnp.broadcast_to(rows[None], (tp_count,) + rows.shape)
    blocks = lax.all_to_all(copies, "tp", 0, 0, tiled=True)
    return blocks.transpose(1, 0, 2).reshape(rows.shape[0], -1)


def shift(value, axis, step):
    size = lax.axis_size(axis)
    return lax.ppermute(value, axis, [(k, (k + step) % size) for k in range(size)])


def ring_gather(value, axis):
    size = lax.axis_size(axis)
    return jnp.stack([value] + [shift(value, axis, -step) for step in range(1, size)], axis=0)


def eight_gather(value, axis):
    from_next = shift(value, axis, -1)
    from_last = shift(value, axis, 1)
    three = jnp.stack([from_last, value, from_next], axis=0)
    far_next = shift(three, axis, -3)
    far_last = shift(three, axis, 3)
    return jnp.stack(
        [value, from_next, far_next[0], far_next[1], far_next[2], far_last[1], far_last[2], from_last],
        axis=0,
    )


def four_gather(value, axis):
    from_next = shift(value, axis, -1)
    from_last = shift(value, axis, 1)
    half = value.shape[-1] // 2
    via_last = shift(from_last[..., :half], axis, 1)
    via_next = shift(from_next[..., half:], axis, -1)
    opposite = jnp.concatenate([via_last, via_next], axis=-1)
    return jnp.stack([value, from_next, opposite, from_last], axis=0)


def gather_plane(shard):
    by_y = eight_gather(shard, "ry") if lax.axis_size("ry") == 8 else ring_gather(shard, "ry")
    return four_gather(by_y, "rx") if lax.axis_size("rx") == 4 else ring_gather(by_y, "rx")


def shards(
    vit_context,
    vision_residual,
    out_weight,
    layer_scale,
    prompt,
    prompt_len,
    image_at,
    grid_sizes,
    image_owner,
    norm_gain,
    qkv_weight,
):
    requests = lax.axis_size(REQ)
    device_index = lax.axis_index(REQ)
    feature_width = vit_context.shape[1]
    merged_context = jnp.mean(
        vit_context.astype(jnp.float32).reshape(-1, 4, feature_width), axis=1
    ).astype(jnp.bfloat16)
    merged_residual = jnp.mean(
        vision_residual.astype(jnp.float32).reshape(-1, 4, feature_width), axis=1
    )
    own_half = gather_plane(out_weight)
    other_half = lax.ppermute(own_half, "rc", [(0, 1), (1, 0)])
    core = lax.axis_index("rc")
    own_part = jnp.einsum(
        "gk,xykn->gxyn", merged_context, own_half, preferred_element_type=jnp.float32
    )
    other_part = jnp.einsum(
        "gk,xykn->gxyn", merged_context, other_half, preferred_element_type=jnp.float32
    )
    partial_value = jnp.stack(
        [jnp.where(core == 0, own_part, other_part), jnp.where(core == 0, other_part, own_part)],
        axis=3,
    ).astype(jnp.bfloat16)
    partial_value = jnp.roll(partial_value, lax.axis_index("rx"), axis=1)
    partial_value = jnp.roll(partial_value, lax.axis_index("ry"), axis=2)
    partial_value = partial_value.reshape(own_part.shape[0], -1)
    tp_count = lax.axis_size("tp")
    block_terms = partial_value.astype(jnp.bfloat16).reshape(
        -1, tp_count, feature_width
    ).transpose(1, 0, 2)
    own_share = jnp.sum(
        lax.all_to_all(block_terms, "tp", 0, 0, tiled=True).astype(jnp.float32), axis=0
    )
    merged = (merged_residual + layer_scale[None, :] * own_share).astype(jnp.bfloat16)
    merged_count = merged.shape[0]
    counts, starts = request_plan(grid_sizes, image_owner, requests)
    request_ends = starts + counts
    capacity = (IMG_MAX + requests - 1) // requests
    request_ids = jnp.arange(requests, dtype=jnp.int32)
    group_index = jnp.arange(merged_count, dtype=jnp.int32) * requests + device_index
    destination = jnp.sum((request_ends[None, :] <= group_index[:, None]).astype(jnp.int32), axis=1)
    owned_start = jnp.sum(
        jnp.where(destination[:, None] == request_ids[None, :], starts[None, :], 0), axis=1
    )
    target = destination * capacity + (group_index - owned_start) // requests
    usable = destination < requests
    send_slots = jnp.arange(requests * capacity, dtype=jnp.int32)
    placing = ((send_slots[:, None] == target[None, :]) & usable[None, :]).astype(jnp.bfloat16)
    outgoing = jnp.dot(placing, merged, preferred_element_type=jnp.float32).astype(jnp.bfloat16)
    arrived = lax.all_to_all(
        outgoing.reshape(requests, capacity, feature_width),
        REQ,
        split_axis=0,
        concat_axis=0,
        tiled=True,
    )
    arrived = arrived.reshape(requests * capacity, feature_width)
    own_request = request_ids == device_index
    own_count = jnp.sum(jnp.where(own_request, counts, 0))
    own_start = jnp.sum(jnp.where(own_request, starts, 0))
    image_from = image_at[0]
    prompt_count = prompt_len[0]
    seq_slots = prompt.shape[1] + IMG_MAX
    slot_index = jnp.arange(seq_slots, dtype=jnp.int32)
    image_row = slot_index - image_from
    in_image = (image_row >= 0) & (image_row < own_count)
    is_live = slot_index < prompt_count + own_count
    from_prompt = is_live & jnp.logical_not(in_image)
    prompt_row = jnp.where(slot_index < image_from, slot_index, slot_index - own_count)
    prompt_ids = jnp.arange(prompt.shape[1], dtype=jnp.int32)
    prompt_pick = ((prompt_row[:, None] == prompt_ids[None, :]) & from_prompt[:, None]).astype(
        jnp.bfloat16
    )
    full_image = gather_features(arrived, tp_count)
    full_prompt = lax.all_gather(prompt[0], "tp", axis=1, tiled=True)
    full_weight = lax.all_gather(qkv_weight, REQ, axis=0, tiled=True)
    cosine_table, sine_table = rope_tables(seq_slots)
    prompt_rows = jnp.dot(prompt_pick, full_prompt, preferred_element_type=jnp.float32)
    prompt_normed = normalize(prompt_rows.astype(jnp.bfloat16), norm_gain)
    prompt_out = apply_rope(
        jnp.dot(prompt_normed, full_weight, preferred_element_type=jnp.float32),
        cosine_table,
        sine_table,
    ).astype(jnp.bfloat16)
    image_ids = jnp.arange(IMG_MAX, dtype=jnp.int32)
    image_flat = (own_start + image_ids) % requests * capacity + image_ids // requests
    image_order = (
        (image_flat[:, None] == send_slots[None, :]) & (image_ids < own_count)[:, None]
    ).astype(jnp.bfloat16)
    full_image, prompt_out = lax.optimization_barrier((full_image, prompt_out))
    image_rows = jnp.dot(image_order, full_image, preferred_element_type=jnp.float32)
    image_normed = normalize(image_rows.astype(jnp.bfloat16), norm_gain)
    image_out = apply_rope(
        jnp.dot(image_normed, full_weight, preferred_element_type=jnp.float32),
        lax.dynamic_slice_in_dim(cosine_table, image_from, IMG_MAX, 0),
        lax.dynamic_slice_in_dim(sine_table, image_from, IMG_MAX, 0),
    ).astype(jnp.bfloat16)
    image_place = ((image_row[:, None] == image_ids[None, :]) & in_image[:, None]).astype(
        jnp.bfloat16
    )
    placed = jnp.dot(image_place, image_out, preferred_element_type=jnp.float32)
    return jnp.where(in_image[:, None], placed.astype(jnp.bfloat16), prompt_out)


def solution(mesh):
    in_specs = (
        P("req", "tp"),
        P("req", "tp"),
        P("tp", "req"),
        P("tp"),
        P("req", None, "tp"),
        P("req"),
        P("req"),
        P(),
        P(),
        P(),
        P("req", "tp"),
    )
    out_specs = P("req", "tp")
    rows, columns = mesh.devices.shape
    x_size = len({device.coords[0] for device in mesh.devices.flat})
    split_mesh = Mesh(
        mesh.devices.reshape(x_size, rows // (2 * x_size), 2, columns), REQ + ("tp",)
    )
    rename = lambda spec: P(*(REQ if axis == "req" else axis for axis in spec))
    return jax.shard_map(
        shards,
        mesh=split_mesh,
        in_specs=tuple(rename(spec) for spec in in_specs),
        out_specs=rename(out_specs),
        check_vma=False,
    )
```

```python
import jax
import jax.numpy as jnp
from jax import lax
from jax.sharding import Mesh, PartitionSpec as P

HEAD = 128
GROUP = 4
IMG_MAX = 128
REQ = ("rx", "ry", "rc")


def request_plan(grid_sizes, image_owner, requests):
    image_rows = grid_sizes[:, 0] * grid_sizes[:, 1]
    member = (image_owner[:, None] == jnp.arange(requests, dtype=jnp.int32)[None, :]).astype(
        jnp.int32
    )
    counts = jnp.sum(image_rows[:, None] * member, axis=0)
    starts = jnp.cumsum(counts) - counts
    return (counts, starts)


def rope_tables(count):
    half_size = HEAD // 2
    exponent = jnp.arange(half_size, dtype=jnp.float32) * (2.0 / HEAD)
    frequency = jnp.exp(-exponent * jnp.log(jnp.float32(500000.0)))
    angles = jnp.arange(count, dtype=jnp.float32)[:, None] * frequency[None, :]
    return (jnp.cos(angles), jnp.sin(angles))


def apply_rope(projected, cosine_table, sine_table):
    seq_rows = projected.shape[0]
    head_blocks = projected.reshape(seq_rows, -1, GROUP + 2, HEAD)
    turning = head_blocks[:, :, : GROUP + 1, :]
    first_half = turning[..., : HEAD // 2]
    second_half = turning[..., HEAD // 2 :]
    cosine_wide = cosine_table[:, None, None, :]
    sine_wide = sine_table[:, None, None, :]
    turned = jnp.concatenate(
        [
            first_half * cosine_wide - second_half * sine_wide,
            second_half * cosine_wide + first_half * sine_wide,
        ],
        axis=-1,
    )
    head_blocks = jnp.concatenate([turned, head_blocks[:, :, GROUP + 1 :, :]], axis=2)
    return head_blocks.reshape(seq_rows, -1)


def normalize(embedded, norm_gain):
    values = embedded.astype(jnp.float32)
    mean_square = jnp.mean(values * values, axis=-1, keepdims=True)
    return (values * lax.rsqrt(mean_square + 1e-05) * norm_gain[None, :]).astype(jnp.bfloat16)


def gather_features(rows, tp_count):
    copies = jnp.broadcast_to(rows[None], (tp_count,) + rows.shape)
    blocks = lax.all_to_all(copies, "tp", 0, 0, tiled=True)
    return blocks.transpose(1, 0, 2).reshape(rows.shape[0], -1)


def shift(value, axis, step):
    size = lax.axis_size(axis)
    return lax.ppermute(value, axis, [(k, (k + step) % size) for k in range(size)])


def ring_gather(value, axis):
    size = lax.axis_size(axis)
    return jnp.stack([value] + [shift(value, axis, -step) for step in range(1, size)], axis=0)


def eight_gather(value, axis):
    from_next = shift(value, axis, -1)
    from_last = shift(value, axis, 1)
    three = jnp.stack([from_last, value, from_next], axis=0)
    far_next = shift(three, axis, -3)
    far_last = shift(three, axis, 3)
    return jnp.stack(
        [value, from_next, far_next[0], far_next[1], far_next[2], far_last[1], far_last[2], from_last],
        axis=0,
    )


def gather_plane(shard):
    by_y = eight_gather(shard, "ry") if lax.axis_size("ry") == 8 else ring_gather(shard, "ry")
    return ring_gather(by_y, "rx")


def shards(
    vit_context,
    vision_residual,
    out_weight,
    layer_scale,
    prompt,
    prompt_len,
    image_at,
    grid_sizes,
    image_owner,
    norm_gain,
    qkv_weight,
):
    requests = lax.axis_size(REQ)
    device_index = lax.axis_index(REQ)
    feature_width = vit_context.shape[1]
    merged_context = jnp.mean(
        vit_context.astype(jnp.float32).reshape(-1, 4, feature_width), axis=1
    ).astype(jnp.bfloat16)
    merged_residual = jnp.mean(
        vision_residual.astype(jnp.float32).reshape(-1, 4, feature_width), axis=1
    )
    own_half = gather_plane(out_weight)
    other_half = lax.ppermute(own_half, "rc", [(0, 1), (1, 0)])
    core = lax.axis_index("rc")
    own_part = jnp.einsum(
        "gk,xykn->gxyn", merged_context, own_half, preferred_element_type=jnp.float32
    )
    other_part = jnp.einsum(
        "gk,xykn->gxyn", merged_context, other_half, preferred_element_type=jnp.float32
    )
    partial_value = jnp.stack(
        [jnp.where(core == 0, own_part, other_part), jnp.where(core == 0, other_part, own_part)],
        axis=3,
    ).astype(jnp.bfloat16)
    partial_value = jnp.roll(partial_value, lax.axis_index("rx"), axis=1)
    partial_value = jnp.roll(partial_value, lax.axis_index("ry"), axis=2)
    partial_value = partial_value.reshape(own_part.shape[0], -1)
    tp_count = lax.axis_size("tp")
    block_terms = partial_value.astype(jnp.bfloat16).reshape(
        -1, tp_count, feature_width
    ).transpose(1, 0, 2)
    own_share = jnp.sum(
        lax.all_to_all(block_terms, "tp", 0, 0, tiled=True).astype(jnp.float32), axis=0
    )
    merged = (merged_residual + layer_scale[None, :] * own_share).astype(jnp.bfloat16)
    merged_count = merged.shape[0]
    counts, starts = request_plan(grid_sizes, image_owner, requests)
    request_ends = starts + counts
    capacity = (IMG_MAX + requests - 1) // requests
    request_ids = jnp.arange(requests, dtype=jnp.int32)
    group_index = jnp.arange(merged_count, dtype=jnp.int32) * requests + device_index
    destination = jnp.sum((request_ends[None, :] <= group_index[:, None]).astype(jnp.int32), axis=1)
    owned_start = jnp.sum(
        jnp.where(destination[:, None] == request_ids[None, :], starts[None, :], 0), axis=1
    )
    target = destination * capacity + (group_index - owned_start) // requests
    usable = destination < requests
    send_slots = jnp.arange(requests * capacity, dtype=jnp.int32)
    placing = ((send_slots[:, None] == target[None, :]) & usable[None, :]).astype(jnp.bfloat16)
    outgoing = jnp.dot(placing, merged, preferred_element_type=jnp.float32).astype(jnp.bfloat16)
    arrived = lax.all_to_all(
        outgoing.reshape(requests, capacity, feature_width),
        REQ,
        split_axis=0,
        concat_axis=0,
        tiled=True,
    )
    arrived = arrived.reshape(requests * capacity, feature_width)
    own_request = request_ids == device_index
    own_count = jnp.sum(jnp.where(own_request, counts, 0))
    own_start = jnp.sum(jnp.where(own_request, starts, 0))
    image_from = image_at[0]
    prompt_count = prompt_len[0]
    seq_slots = prompt.shape[1] + IMG_MAX
    slot_index = jnp.arange(seq_slots, dtype=jnp.int32)
    image_row = slot_index - image_from
    in_image = (image_row >= 0) & (image_row < own_count)
    is_live = slot_index < prompt_count + own_count
    from_prompt = is_live & jnp.logical_not(in_image)
    prompt_row = jnp.where(slot_index < image_from, slot_index, slot_index - own_count)
    prompt_ids = jnp.arange(prompt.shape[1], dtype=jnp.int32)
    prompt_pick = ((prompt_row[:, None] == prompt_ids[None, :]) & from_prompt[:, None]).astype(
        jnp.bfloat16
    )
    full_image = lax.all_gather(arrived, "tp", axis=1, tiled=True)
    full_prompt = lax.all_gather(prompt[0], "tp", axis=1, tiled=True)
    full_weight = lax.all_gather(qkv_weight, REQ, axis=0, tiled=True)
    cosine_table, sine_table = rope_tables(seq_slots)
    prompt_rows = jnp.dot(prompt_pick, full_prompt, preferred_element_type=jnp.float32)
    prompt_normed = normalize(prompt_rows.astype(jnp.bfloat16), norm_gain)
    prompt_out = apply_rope(
        jnp.dot(prompt_normed, full_weight, preferred_element_type=jnp.float32),
        cosine_table,
        sine_table,
    ).astype(jnp.bfloat16)
    image_ids = jnp.arange(IMG_MAX, dtype=jnp.int32)
    image_flat = (own_start + image_ids) % requests * capacity + image_ids // requests
    image_order = (
        (image_flat[:, None] == send_slots[None, :]) & (image_ids < own_count)[:, None]
    ).astype(jnp.bfloat16)
    full_image, prompt_out = lax.optimization_barrier((full_image, prompt_out))
    image_rows = jnp.dot(image_order, full_image, preferred_element_type=jnp.float32)
    image_normed = normalize(image_rows.astype(jnp.bfloat16), norm_gain)
    image_out = apply_rope(
        jnp.dot(image_normed, full_weight, preferred_element_type=jnp.float32),
        lax.dynamic_slice_in_dim(cosine_table, image_from, IMG_MAX, 0),
        lax.dynamic_slice_in_dim(sine_table, image_from, IMG_MAX, 0),
    ).astype(jnp.bfloat16)
    image_place = ((image_row[:, None] == image_ids[None, :]) & in_image[:, None]).astype(
        jnp.bfloat16
    )
    placed = jnp.dot(image_place, image_out, preferred_element_type=jnp.float32)
    return jnp.where(in_image[:, None], placed.astype(jnp.bfloat16), prompt_out)


def solution(mesh):
    in_specs = (
        P("req", "tp"),
        P("req", "tp"),
        P("tp", "req"),
        P("tp"),
        P("req", None, "tp"),
        P("req"),
        P("req"),
        P(),
        P(),
        P(),
        P("req", "tp"),
    )
    out_specs = P("req", "tp")
    rows, columns = mesh.devices.shape
    x_size = len({device.coords[0] for device in mesh.devices.flat})
    split_mesh = Mesh(
        mesh.devices.reshape(x_size, rows // (2 * x_size), 2, columns), REQ + ("tp",)
    )
    rename = lambda spec: P(*(REQ if axis == "req" else axis for axis in spec))
    return jax.shard_map(
        shards,
        mesh=split_mesh,
        in_specs=tuple(rename(spec) for spec in in_specs),
        out_specs=rename(out_specs),
        check_vma=False,
    )
```

```python
import jax
import jax.numpy as jnp
from jax import lax
from jax.sharding import Mesh, PartitionSpec as P

HEAD = 128
GROUP = 4
IMG_MAX = 128
REQ = ("rx", "ry", "rc")


def request_plan(grid_sizes, image_owner, requests):
    image_rows = grid_sizes[:, 0] * grid_sizes[:, 1]
    member = (image_owner[:, None] == jnp.arange(requests, dtype=jnp.int32)[None, :]).astype(
        jnp.int32
    )
    counts = jnp.sum(image_rows[:, None] * member, axis=0)
    starts = jnp.cumsum(counts) - counts
    return (counts, starts)


def rope_tables(count):
    half_size = HEAD // 2
    exponent = jnp.arange(half_size, dtype=jnp.float32) * (2.0 / HEAD)
    frequency = jnp.exp(-exponent * jnp.log(jnp.float32(500000.0)))
    angles = jnp.arange(count, dtype=jnp.float32)[:, None] * frequency[None, :]
    return (jnp.cos(angles), jnp.sin(angles))


def apply_rope(projected, cosine_table, sine_table):
    seq_rows = projected.shape[0]
    head_blocks = projected.reshape(seq_rows, -1, GROUP + 2, HEAD)
    turning = head_blocks[:, :, : GROUP + 1, :]
    first_half = turning[..., : HEAD // 2]
    second_half = turning[..., HEAD // 2 :]
    cosine_wide = cosine_table[:, None, None, :]
    sine_wide = sine_table[:, None, None, :]
    turned = jnp.concatenate(
        [
            first_half * cosine_wide - second_half * sine_wide,
            second_half * cosine_wide + first_half * sine_wide,
        ],
        axis=-1,
    )
    head_blocks = jnp.concatenate([turned, head_blocks[:, :, GROUP + 1 :, :]], axis=2)
    return head_blocks.reshape(seq_rows, -1)


def normalize(embedded, norm_gain):
    values = embedded.astype(jnp.float32)
    mean_square = jnp.mean(values * values, axis=-1, keepdims=True)
    return (values * lax.rsqrt(mean_square + 1e-05) * norm_gain[None, :]).astype(jnp.bfloat16)


def gather_features(rows, tp_count):
    copies = jnp.broadcast_to(rows[None], (tp_count,) + rows.shape)
    blocks = lax.all_to_all(copies, "tp", 0, 0, tiled=True)
    return blocks.transpose(1, 0, 2).reshape(rows.shape[0], -1)


def shift(value, axis, step):
    size = lax.axis_size(axis)
    return lax.ppermute(value, axis, [(k, (k + step) % size) for k in range(size)])


def ring_gather(value, axis):
    size = lax.axis_size(axis)
    return jnp.stack([value] + [shift(value, axis, -step) for step in range(1, size)], axis=0)


def eight_gather(value, axis):
    from_next = shift(value, axis, -1)
    from_last = shift(value, axis, 1)
    three = jnp.stack([from_last, value, from_next], axis=0)
    far_next = shift(three, axis, -3)
    far_last = shift(three, axis, 3)
    return jnp.stack(
        [value, from_next, far_next[0], far_next[1], far_next[2], far_last[1], far_last[2], from_last],
        axis=0,
    )


def gather_plane(shard):
    by_y = eight_gather(shard, "ry") if lax.axis_size("ry") == 8 else ring_gather(shard, "ry")
    return ring_gather(by_y, "rx")


def shards(
    vit_context,
    vision_residual,
    out_weight,
    layer_scale,
    prompt,
    prompt_len,
    image_at,
    grid_sizes,
    image_owner,
    norm_gain,
    qkv_weight,
):
    requests = lax.axis_size(REQ)
    device_index = lax.axis_index(REQ)
    feature_width = vit_context.shape[1]
    merged_context = jnp.mean(
        vit_context.astype(jnp.float32).reshape(-1, 4, feature_width), axis=1
    ).astype(jnp.bfloat16)
    merged_residual = jnp.mean(
        vision_residual.astype(jnp.float32).reshape(-1, 4, feature_width), axis=1
    )
    own_half = gather_plane(out_weight)
    partner_context = lax.ppermute(merged_context, "rc", [(0, 1), (1, 0)])
    core = lax.axis_index("rc")
    own_part = jnp.einsum(
        "gk,xykn->gxyn", merged_context, own_half, preferred_element_type=jnp.float32
    ).astype(jnp.bfloat16)
    partner_part = jnp.einsum(
        "gk,xykn->gxyn", partner_context, own_half, preferred_element_type=jnp.float32
    ).astype(jnp.bfloat16)
    other_part = lax.ppermute(partner_part, "rc", [(0, 1), (1, 0)])
    partial_value = jnp.stack(
        [jnp.where(core == 0, own_part, other_part), jnp.where(core == 0, other_part, own_part)],
        axis=3,
    ).astype(jnp.bfloat16)
    partial_value = jnp.roll(partial_value, lax.axis_index("rx"), axis=1)
    partial_value = jnp.roll(partial_value, lax.axis_index("ry"), axis=2)
    partial_value = partial_value.reshape(own_part.shape[0], -1)
    tp_count = lax.axis_size("tp")
    block_terms = partial_value.astype(jnp.bfloat16).reshape(
        -1, tp_count, feature_width
    ).transpose(1, 0, 2)
    own_share = jnp.sum(
        lax.all_to_all(block_terms, "tp", 0, 0, tiled=True).astype(jnp.float32), axis=0
    )
    merged = (merged_residual + layer_scale[None, :] * own_share).astype(jnp.bfloat16)
    merged_count = merged.shape[0]
    counts, starts = request_plan(grid_sizes, image_owner, requests)
    request_ends = starts + counts
    capacity = (IMG_MAX + requests - 1) // requests
    request_ids = jnp.arange(requests, dtype=jnp.int32)
    group_index = jnp.arange(merged_count, dtype=jnp.int32) * requests + device_index
    destination = jnp.sum((request_ends[None, :] <= group_index[:, None]).astype(jnp.int32), axis=1)
    owned_start = jnp.sum(
        jnp.where(destination[:, None] == request_ids[None, :], starts[None, :], 0), axis=1
    )
    target = destination * capacity + (group_index - owned_start) // requests
    usable = destination < requests
    send_slots = jnp.arange(requests * capacity, dtype=jnp.int32)
    placing = ((send_slots[:, None] == target[None, :]) & usable[None, :]).astype(jnp.bfloat16)
    outgoing = jnp.dot(placing, merged, preferred_element_type=jnp.float32).astype(jnp.bfloat16)
    arrived = lax.all_to_all(
        outgoing.reshape(requests, capacity, feature_width),
        REQ,
        split_axis=0,
        concat_axis=0,
        tiled=True,
    )
    arrived = arrived.reshape(requests * capacity, feature_width)
    own_request = request_ids == device_index
    own_count = jnp.sum(jnp.where(own_request, counts, 0))
    own_start = jnp.sum(jnp.where(own_request, starts, 0))
    image_from = image_at[0]
    prompt_count = prompt_len[0]
    seq_slots = prompt.shape[1] + IMG_MAX
    slot_index = jnp.arange(seq_slots, dtype=jnp.int32)
    image_row = slot_index - image_from
    in_image = (image_row >= 0) & (image_row < own_count)
    is_live = slot_index < prompt_count + own_count
    from_prompt = is_live & jnp.logical_not(in_image)
    prompt_row = jnp.where(slot_index < image_from, slot_index, slot_index - own_count)
    prompt_ids = jnp.arange(prompt.shape[1], dtype=jnp.int32)
    prompt_pick = ((prompt_row[:, None] == prompt_ids[None, :]) & from_prompt[:, None]).astype(
        jnp.bfloat16
    )
    full_image = gather_features(arrived, tp_count)
    full_prompt = lax.all_gather(prompt[0], "tp", axis=1, tiled=True)
    full_weight = lax.all_gather(qkv_weight, REQ, axis=0, tiled=True)
    cosine_table, sine_table = rope_tables(seq_slots)
    prompt_rows = jnp.dot(prompt_pick, full_prompt, preferred_element_type=jnp.float32)
    prompt_normed = normalize(prompt_rows.astype(jnp.bfloat16), norm_gain)
    prompt_out = apply_rope(
        jnp.dot(prompt_normed, full_weight, preferred_element_type=jnp.float32),
        cosine_table,
        sine_table,
    ).astype(jnp.bfloat16)
    image_ids = jnp.arange(IMG_MAX, dtype=jnp.int32)
    image_flat = (own_start + image_ids) % requests * capacity + image_ids // requests
    image_order = (
        (image_flat[:, None] == send_slots[None, :]) & (image_ids < own_count)[:, None]
    ).astype(jnp.bfloat16)
    full_image, prompt_out = lax.optimization_barrier((full_image, prompt_out))
    image_rows = jnp.dot(image_order, full_image, preferred_element_type=jnp.float32)
    image_normed = normalize(image_rows.astype(jnp.bfloat16), norm_gain)
    image_out = apply_rope(
        jnp.dot(image_normed, full_weight, preferred_element_type=jnp.float32),
        lax.dynamic_slice_in_dim(cosine_table, image_from, IMG_MAX, 0),
        lax.dynamic_slice_in_dim(sine_table, image_from, IMG_MAX, 0),
    ).astype(jnp.bfloat16)
    image_place = ((image_row[:, None] == image_ids[None, :]) & in_image[:, None]).astype(
        jnp.bfloat16
    )
    placed = jnp.dot(image_place, image_out, preferred_element_type=jnp.float32)
    return jnp.where(in_image[:, None], placed.astype(jnp.bfloat16), prompt_out)


def solution(mesh):
    in_specs = (
        P("req", "tp"),
        P("req", "tp"),
        P("tp", "req"),
        P("tp"),
        P("req", None, "tp"),
        P("req"),
        P("req"),
        P(),
        P(),
        P(),
        P("req", "tp"),
    )
    out_specs = P("req", "tp")
    rows, columns = mesh.devices.shape
    x_size = len({device.coords[0] for device in mesh.devices.flat})
    split_mesh = Mesh(
        mesh.devices.reshape(x_size, rows // (2 * x_size), 2, columns), REQ + ("tp",)
    )
    rename = lambda spec: P(*(REQ if axis == "req" else axis for axis in spec))
    return jax.shard_map(
        shards,
        mesh=split_mesh,
        in_specs=tuple(rename(spec) for spec in in_specs),
        out_specs=rename(out_specs),
        check_vma=False,
    )
```

```python
import jax
import jax.numpy as jnp
from jax import lax
from jax.sharding import Mesh, PartitionSpec as P

HEAD = 128
GROUP = 4
IMG_MAX = 128
REQ = ("rx", "ry", "rc")


def request_plan(grid_sizes, image_owner, requests):
    image_rows = grid_sizes[:, 0] * grid_sizes[:, 1]
    member = (image_owner[:, None] == jnp.arange(requests, dtype=jnp.int32)[None, :]).astype(
        jnp.int32
    )
    counts = jnp.sum(image_rows[:, None] * member, axis=0)
    starts = jnp.cumsum(counts) - counts
    return (counts, starts)


def rope_tables(count):
    half_size = HEAD // 2
    exponent = jnp.arange(half_size, dtype=jnp.float32) * (2.0 / HEAD)
    frequency = jnp.exp(-exponent * jnp.log(jnp.float32(500000.0)))
    angles = jnp.arange(count, dtype=jnp.float32)[:, None] * frequency[None, :]
    return (jnp.cos(angles), jnp.sin(angles))


def apply_rope(projected, cosine_table, sine_table):
    seq_rows = projected.shape[0]
    head_blocks = projected.reshape(seq_rows, -1, GROUP + 2, HEAD)
    turning = head_blocks[:, :, : GROUP + 1, :]
    first_half = turning[..., : HEAD // 2]
    second_half = turning[..., HEAD // 2 :]
    cosine_wide = cosine_table[:, None, None, :]
    sine_wide = sine_table[:, None, None, :]
    turned = jnp.concatenate(
        [
            first_half * cosine_wide - second_half * sine_wide,
            second_half * cosine_wide + first_half * sine_wide,
        ],
        axis=-1,
    )
    head_blocks = jnp.concatenate([turned, head_blocks[:, :, GROUP + 1 :, :]], axis=2)
    return head_blocks.reshape(seq_rows, -1)


def normalize(embedded, norm_gain):
    values = embedded.astype(jnp.float32)
    mean_square = jnp.mean(values * values, axis=-1, keepdims=True)
    return (values * lax.rsqrt(mean_square + 1e-05) * norm_gain[None, :]).astype(jnp.bfloat16)


def gather_features(rows, tp_count):
    copies = jnp.broadcast_to(rows[None], (tp_count,) + rows.shape)
    blocks = lax.all_to_all(copies, "tp", 0, 0, tiled=True)
    return blocks.transpose(1, 0, 2).reshape(rows.shape[0], -1)


def shift(value, axis, step):
    size = lax.axis_size(axis)
    return lax.ppermute(value, axis, [(k, (k + step) % size) for k in range(size)])


def ring_gather(value, axis):
    size = lax.axis_size(axis)
    return jnp.stack([value] + [shift(value, axis, -step) for step in range(1, size)], axis=0)


def eight_gather(value, axis):
    from_next = shift(value, axis, -1)
    from_last = shift(value, axis, 1)
    three = jnp.stack([from_last, value, from_next], axis=0)
    far_next = shift(three, axis, -3)
    far_last = shift(three, axis, 3)
    return jnp.stack(
        [value, from_next, far_next[0], far_next[1], far_next[2], far_last[1], far_last[2], from_last],
        axis=0,
    )


def gather_plane(shard):
    by_y = eight_gather(shard, "ry") if lax.axis_size("ry") == 8 else ring_gather(shard, "ry")
    return ring_gather(by_y, "rx")


def shards(
    vit_context,
    vision_residual,
    out_weight,
    layer_scale,
    prompt,
    prompt_len,
    image_at,
    grid_sizes,
    image_owner,
    norm_gain,
    qkv_weight,
):
    requests = lax.axis_size(REQ)
    device_index = lax.axis_index(REQ)
    feature_width = vit_context.shape[1]
    merged_context = jnp.mean(
        vit_context.astype(jnp.float32).reshape(-1, 4, feature_width), axis=1
    ).astype(jnp.bfloat16)
    merged_residual = jnp.mean(
        vision_residual.astype(jnp.float32).reshape(-1, 4, feature_width), axis=1
    )
    swap = [(0, 1), (1, 0)]
    core = lax.axis_index("rc")
    context_pair = jnp.stack([merged_context, lax.ppermute(merged_context, "rc", swap)])
    context_ring = ring_gather(context_pair, "rx")
    weight_ring = eight_gather(out_weight, "ry") if lax.axis_size("ry") == 8 else ring_gather(out_weight, "ry")
    parts = jnp.einsum(
        "dcgk,ykn->dcgyn", context_ring, weight_ring, preferred_element_type=jnp.float32
    ).astype(jnp.bfloat16)
    from_partner = lax.ppermute(parts[:, 1], "rc", swap)
    both = jnp.stack([parts[:, 0], from_partner], axis=-2)
    x_count = lax.axis_size("rx")
    landed = [both[0]] + [shift(both[(x_count - d) % x_count], "rx", (x_count - d) % x_count) for d in range(1, x_count)]
    partial_value = jnp.moveaxis(jnp.stack(landed, axis=0), 0, 1)
    partial_value = jnp.where(core == 0, partial_value, partial_value[..., ::-1, :])
    partial_value = jnp.roll(partial_value, lax.axis_index("rx"), axis=1)
    partial_value = jnp.roll(partial_value, lax.axis_index("ry"), axis=2)
    own_part = merged_context
    partial_value = partial_value.reshape(own_part.shape[0], -1)
    tp_count = lax.axis_size("tp")
    block_terms = partial_value.astype(jnp.bfloat16).reshape(
        -1, tp_count, feature_width
    ).transpose(1, 0, 2)
    own_share = jnp.sum(
        lax.all_to_all(block_terms, "tp", 0, 0, tiled=True).astype(jnp.float32), axis=0
    )
    merged = (merged_residual + layer_scale[None, :] * own_share).astype(jnp.bfloat16)
    merged_count = merged.shape[0]
    counts, starts = request_plan(grid_sizes, image_owner, requests)
    request_ends = starts + counts
    capacity = (IMG_MAX + requests - 1) // requests
    request_ids = jnp.arange(requests, dtype=jnp.int32)
    group_index = jnp.arange(merged_count, dtype=jnp.int32) * requests + device_index
    destination = jnp.sum((request_ends[None, :] <= group_index[:, None]).astype(jnp.int32), axis=1)
    owned_start = jnp.sum(
        jnp.where(destination[:, None] == request_ids[None, :], starts[None, :], 0), axis=1
    )
    target = destination * capacity + (group_index - owned_start) // requests
    usable = destination < requests
    send_slots = jnp.arange(requests * capacity, dtype=jnp.int32)
    placing = ((send_slots[:, None] == target[None, :]) & usable[None, :]).astype(jnp.bfloat16)
    outgoing = jnp.dot(placing, merged, preferred_element_type=jnp.float32).astype(jnp.bfloat16)
    arrived = lax.all_to_all(
        outgoing.reshape(requests, capacity, feature_width),
        REQ,
        split_axis=0,
        concat_axis=0,
        tiled=True,
    )
    arrived = arrived.reshape(requests * capacity, feature_width)
    own_request = request_ids == device_index
    own_count = jnp.sum(jnp.where(own_request, counts, 0))
    own_start = jnp.sum(jnp.where(own_request, starts, 0))
    image_from = image_at[0]
    prompt_count = prompt_len[0]
    seq_slots = prompt.shape[1] + IMG_MAX
    slot_index = jnp.arange(seq_slots, dtype=jnp.int32)
    image_row = slot_index - image_from
    in_image = (image_row >= 0) & (image_row < own_count)
    is_live = slot_index < prompt_count + own_count
    from_prompt = is_live & jnp.logical_not(in_image)
    prompt_row = jnp.where(slot_index < image_from, slot_index, slot_index - own_count)
    prompt_ids = jnp.arange(prompt.shape[1], dtype=jnp.int32)
    prompt_pick = ((prompt_row[:, None] == prompt_ids[None, :]) & from_prompt[:, None]).astype(
        jnp.bfloat16
    )
    full_image = gather_features(arrived, tp_count)
    full_prompt = lax.all_gather(prompt[0], "tp", axis=1, tiled=True)
    full_weight = lax.all_gather(qkv_weight, REQ, axis=0, tiled=True)
    cosine_table, sine_table = rope_tables(seq_slots)
    prompt_rows = jnp.dot(prompt_pick, full_prompt, preferred_element_type=jnp.float32)
    prompt_normed = normalize(prompt_rows.astype(jnp.bfloat16), norm_gain)
    prompt_out = apply_rope(
        jnp.dot(prompt_normed, full_weight, preferred_element_type=jnp.float32),
        cosine_table,
        sine_table,
    ).astype(jnp.bfloat16)
    image_ids = jnp.arange(IMG_MAX, dtype=jnp.int32)
    image_flat = (own_start + image_ids) % requests * capacity + image_ids // requests
    image_order = (
        (image_flat[:, None] == send_slots[None, :]) & (image_ids < own_count)[:, None]
    ).astype(jnp.bfloat16)
    full_image, prompt_out = lax.optimization_barrier((full_image, prompt_out))
    image_rows = jnp.dot(image_order, full_image, preferred_element_type=jnp.float32)
    image_normed = normalize(image_rows.astype(jnp.bfloat16), norm_gain)
    image_out = apply_rope(
        jnp.dot(image_normed, full_weight, preferred_element_type=jnp.float32),
        lax.dynamic_slice_in_dim(cosine_table, image_from, IMG_MAX, 0),
        lax.dynamic_slice_in_dim(sine_table, image_from, IMG_MAX, 0),
    ).astype(jnp.bfloat16)
    image_place = ((image_row[:, None] == image_ids[None, :]) & in_image[:, None]).astype(
        jnp.bfloat16
    )
    placed = jnp.dot(image_place, image_out, preferred_element_type=jnp.float32)
    return jnp.where(in_image[:, None], placed.astype(jnp.bfloat16), prompt_out)


def solution(mesh):
    in_specs = (
        P("req", "tp"),
        P("req", "tp"),
        P("tp", "req"),
        P("tp"),
        P("req", None, "tp"),
        P("req"),
        P("req"),
        P(),
        P(),
        P(),
        P("req", "tp"),
    )
    out_specs = P("req", "tp")
    rows, columns = mesh.devices.shape
    x_size = len({device.coords[0] for device in mesh.devices.flat})
    split_mesh = Mesh(
        mesh.devices.reshape(x_size, rows // (2 * x_size), 2, columns), REQ + ("tp",)
    )
    rename = lambda spec: P(*(REQ if axis == "req" else axis for axis in spec))
    return jax.shard_map(
        shards,
        mesh=split_mesh,
        in_specs=tuple(rename(spec) for spec in in_specs),
        out_specs=rename(out_specs),
        check_vma=False,
    )
```
